512 devices in a mesh: page: 32 (over y_lo, z), req: 16 (over y_hi, x, core).
Axes of the slice: x: 4, y: 8 (y_hi: 2, y_lo: 4; y = y_hi * 4 + y_lo), z: 8, core: 2. Of those that a mesh axis runs over, the one named last changes fastest.
Arguments:
- queries: bfloat16 [256, 8192], P('req'), may hold values from -250 to 250
- key_pool: bfloat16 [512, 128, 1024], P(('page', 'req')), may hold values from -6 to 6
- value_pool: bfloat16 [512, 128, 1024], P(('page', 'req')), may hold values from -6 to 6
- page_table: int32 [256, 32], P('req'), may hold values from 0 to 511, as said below
- page_count: int32 [256], P('req'), may hold values from 1 to 32, as said below
Outputs:
- attended: bfloat16 [256, 8192], P('req', 'page')
The draws below stay inside these ranges and needn't reach their ends.
Inputs may be any that keep to these rules, and one draw needn't show every extreme that they name: `page_table`: rows of a request's table up to page_count are distinct pages; slots beyond it hold 0 and are not part of the context. `page_count`: some request has 32 live slots and some has one.
All inputs are finite; a program needn't handle non-finite values.
Results may differ from the reference program's by a relative error of at most 0.013.
Values may be sent and summed in bfloat16 or wider, within the bound.
No kernel may reach another device: no remote copies, remote signals or barrier semaphores. Data moves between devices by JAX's collectives and lax.ppermute only.
A program may use at most 64 MiB of HBM per device.

```python
import math
import jax
import jax.numpy as jnp
from jax import lax

H = 64
KVH = 8
HD = 128
PAGE = 128
MAXP = 32
NPAGES = 512
REQUESTS = 256
PREF = 16
BRANCH = 16


def table_common(key):
    first_key, second_key, third_key, fourth_key = jax.random.split(jax.random.fold_in(key, 7), 4)
    shuffled = jax.random.permutation(first_key, NPAGES)
    branch_pick = jnp.minimum(jax.random.randint(second_key, (REQUESTS,), 0, BRANCH), jax.random.randint(third_key, (REQUESTS,), 0, BRANCH))
    position = jnp.arange(MAXP, dtype=jnp.int32)[None, :]
    row_index = jnp.arange(REQUESTS, dtype=jnp.int32)[:, None]
    private_slots = MAXP - PREF
    region = NPAGES - BRANCH * PREF
    raw_ids = jnp.where(position < PREF, branch_pick[:, None] * PREF + position, BRANCH * PREF + (row_index * private_slots + position - PREF) % region)
    page_ids = shuffled[raw_ids]
    live_count = jax.random.randint(fourth_key, (REQUESTS,), 1, MAXP + 1)
    live_count = live_count.at[0].set(MAXP).at[REQUESTS - 1].set(1)
    page_ids = jnp.where(position < live_count[:, None], page_ids, 0)
    return (page_ids.astype(jnp.int32), live_count.astype(jnp.int32))


def draw_page_table(key, part):
    return table_common(key)[0]


def draw_page_count(key, part):
    return table_common(key)[1]


def draw_queries(key, part):
    normal_base = jax.random.normal(key, (REQUESTS, H * HD), jnp.float32)
    drawn = jnp.clip(normal_base, -6.0, 6.0)
    return drawn.astype(jnp.bfloat16)


def steps_of(key, dims, pieces, low, largest):
    loudness = 1.0
    for axis_at, blocks in pieces:
        heights = jax.random.uniform(jax.random.fold_in(jax.random.fold_in(key, 6), axis_at), (blocks,), jnp.float32, low / len(pieces), largest / len(pieces))
        loudness = loudness * jnp.repeat(jnp.exp(heights), dims[axis_at] // blocks).reshape((-1,) + (1,) * (len(dims) - 1 - axis_at))
    return loudness


def bell_draw(key, extent, deviation, reach, cuts=(), held_as=jnp.bfloat16):
    array = deviation * jax.random.normal(key, extent, jnp.float32)
    if cuts:
        array = array * steps_of(key, extent, cuts, -0.22, 0.18)
    return jnp.clip(array, -reach, reach).astype(held_as)


def setup_inputs(seed: int = 0) -> dict:
    streams_of = jax.random.split(jax.random.key(seed), 6)
    queries = draw_queries(jax.random.fold_in(streams_of[5], 71), 0)
    key_pool = bell_draw(streams_of[1], (NPAGES, PAGE, KVH * HD), 1.0, 6.0, ((0, 512),))
    value_pool = bell_draw(streams_of[2], (NPAGES, PAGE, KVH * HD), 1.0, 6.0, ((0, 512),))
    page_table = draw_page_table(jax.random.fold_in(streams_of[5], 71), 0)
    page_count = draw_page_count(jax.random.fold_in(streams_of[5], 71), 0)
    return dict(queries=queries, key_pool=key_pool, value_pool=value_pool, page_table=page_table, page_count=page_count)


def reference(queries, key_pool, value_pool, page_table, page_count):
    score_scale = 1.0 / math.sqrt(HD)
    per_kv = H // KVH

    def one_request(inputs):
        query_row, page_ids, live_count = inputs
        key_rows = key_pool[page_ids].reshape(MAXP * PAGE, KVH, HD).astype(jnp.float32)
        value_rows = value_pool[page_ids].reshape(MAXP * PAGE, KVH, HD).astype(jnp.float32)
        grouped = query_row.reshape(KVH, per_kv, HD).astype(jnp.float32)
        scores = jnp.einsum('kgd,tkd->kgt', grouped, key_rows, precision=lax.Precision.HIGHEST) * score_scale
        slot_live = jnp.arange(MAXP) < live_count
        token_live = jnp.repeat(slot_live, PAGE)[None, None, :]
        scores = jnp.where(token_live, scores, jnp.float32(-1e+30))
        row_top = lax.optimization_barrier(jnp.max(scores, axis=2, keepdims=True))
        exp_terms = jnp.where(token_live, jnp.exp(scores - row_top), jnp.float32(0.0))
        totals = lax.optimization_barrier(jnp.sum(exp_terms, axis=2))
        weights = lax.optimization_barrier(exp_terms.astype(jnp.bfloat16)).astype(jnp.float32)
        mixed = jnp.einsum('kgt,tkd->kgd', weights, value_rows, precision=lax.Precision.HIGHEST)
        mixed = mixed / totals[:, :, None]
        return mixed.reshape(H * HD).astype(jnp.bfloat16)
    return lax.map(one_request, (queries, page_table, page_count))
```

```python
import math

import jax
import jax.numpy as jnp
from jax import lax
from jax.sharding import Mesh
from jax.sharding import PartitionSpec as P

H = 64
KVH = 8
HD = 128


def body(queries, key_pool, value_pool, page_table, page_count):
    n_page = lax.axis_size("page")
    n_yh = lax.axis_size("yh")
    n_xc = lax.axis_size("xc")
    page_index = lax.axis_index("page")
    yh_index = lax.axis_index("yh")
    pages_held = key_pool.shape[0]
    page_len = key_pool.shape[1]
    per_kv = H // KVH
    own_heads = H // n_page
    rows = queries.shape[0]
    score_scale = 1.0 / math.sqrt(HD)

    all_q = lax.all_gather(queries, "yh", tiled=True)
    all_table = lax.all_gather(page_table, "yh", tiled=True)
    all_count = lax.all_gather(page_count, "yh", tiled=True)
    keys = lax.all_gather(key_pool, "xc", tiled=True)
    values = lax.all_gather(value_pool, "xc", tiled=True)

    req_rows = all_q.shape[0]
    first_page = (page_index * n_yh + yh_index) * n_xc * pages_held
    held_ids = first_page + jnp.arange(n_xc * pages_held, dtype=jnp.int32)
    slot_live = jnp.arange(all_table.shape[1], dtype=jnp.int32)[None, :] < all_count[:, None]
    page_hit = jnp.any(
        (all_table[:, :, None] == held_ids[None, None, :]) & slot_live[:, :, None], axis=1
    )
    token_hit = jnp.repeat(page_hit, page_len, axis=1)[:, None, None, :]

    grouped = all_q.reshape(req_rows, KVH, per_kv, HD)
    token_keys = keys.reshape(-1, KVH, HD)
    token_values = values.reshape(-1, KVH, HD)
    scores = (
        jnp.einsum("rkgd,tkd->rkgt", grouped, token_keys, preferred_element_type=jnp.float32)
        * score_scale
    )
    scores = jnp.where(token_hit, scores, jnp.float32(-1e30))
    local_max = jnp.max(scores, axis=3)
    global_max = lax.pmax(local_max, ("page", "yh"))
    exp_terms = jnp.where(token_hit, jnp.exp(scores - local_max[..., None]), jnp.float32(0.0))
    local_sum = jnp.sum(exp_terms, axis=3)
    weights = exp_terms.astype(jnp.bfloat16)
    local_out = jnp.einsum(
        "rkgt,tkd->rkgd", weights, token_values, preferred_element_type=jnp.float32
    )
    factor = jnp.exp(local_max - global_max)
    local_out = local_out * factor[..., None]
    local_sum = local_sum * factor

    out_blocks = local_out.reshape(n_yh, rows, n_page, own_heads, HD).transpose(2, 0, 1, 3, 4)
    out_blocks = out_blocks.reshape(n_page * n_yh, rows, own_heads, HD)
    sum_blocks = local_sum.reshape(n_yh, rows, n_page, own_heads).transpose(2, 0, 1, 3)
    sum_blocks = sum_blocks.reshape(n_page * n_yh, rows, own_heads)
    out_red = lax.psum_scatter(out_blocks, ("page", "yh"), scatter_dimension=0, tiled=True)
    sum_red = lax.psum_scatter(sum_blocks, ("page", "yh"), scatter_dimension=0, tiled=True)
    result = out_red[0] / sum_red[0][..., None]
    return result.reshape(rows, own_heads * HD).astype(jnp.bfloat16)


def solution(mesh):
    n_page, n_req = mesh.devices.shape
    n_yh = 2 if n_req % 2 == 0 else 1
    split = Mesh(mesh.devices.reshape(n_page, n_yh, n_req // n_yh), ("page", "yh", "xc"))
    req = ("yh", "xc")
    return jax.shard_map(
        body,
        mesh=split,
        in_specs=(
            P(req, None),
            P(("page",) + req, None, None),
            P(("page",) + req, None, None),
            P(req, None),
            P(req),
        ),
        out_specs=P(req, "page"),
        check_vma=False,
    )
```

```python
import math

import jax
import jax.numpy as jnp
from jax import lax
from jax.sharding import Mesh
from jax.sharding import PartitionSpec as P

H = 64
KVH = 8
HD = 128
LANES = 128


def body(queries, key_pool, value_pool, page_table, page_count):
    n_page = lax.axis_size("page")
    n_yh = lax.axis_size("yh")
    n_xc = lax.axis_size("xc")
    page_index = lax.axis_index("page")
    yh_index = lax.axis_index("yh")
    pages_held = key_pool.shape[0]
    page_len = key_pool.shape[1]
    per_kv = H // KVH
    own_heads = H // n_page
    rows = queries.shape[0]
    score_scale = 1.0 / math.sqrt(HD)

    row_pages = n_yh * n_xc * pages_held
    row_ids = page_index * row_pages + jnp.arange(row_pages, dtype=jnp.int32)
    slot_live = jnp.arange(page_table.shape[1], dtype=jnp.int32)[None, :] < page_count[:, None]
    row_hit = jnp.any(
        (page_table[:, :, None] == row_ids[None, None, :]) & slot_live[:, :, None], axis=1
    )
    mask_cols = -(-row_pages // LANES) * LANES
    row_hit = jnp.pad(row_hit.astype(queries.dtype), ((0, 0), (0, mask_cols - row_pages)))
    packed = jnp.concatenate([queries, row_hit], axis=1)

    all_packed = lax.all_gather(packed, "yh", tiled=True)
    keys = lax.all_gather(key_pool, "xc", tiled=True)
    values = lax.all_gather(value_pool, "xc", tiled=True)

    req_rows = all_packed.shape[0]
    all_q = all_packed[:, : H * HD]
    held = n_xc * pages_held
    page_hit = lax.dynamic_slice_in_dim(all_packed, H * HD + yh_index * held, held, 1) > 0.5
    token_hit = jnp.repeat(page_hit, page_len, axis=1)[:, None, None, :]

    grouped = all_q.reshape(req_rows, KVH, per_kv, HD)
    token_keys = keys.reshape(-1, KVH, HD)
    token_values = values.reshape(-1, KVH, HD)
    scores = (
        jnp.einsum("rkgd,tkd->rkgt", grouped, token_keys, preferred_element_type=jnp.float32)
        * score_scale
    )
    scores = jnp.where(token_hit, scores, jnp.float32(-1e30))
    local_max = jnp.max(scores, axis=3)
    exp_terms = jnp.where(token_hit, jnp.exp(scores - local_max[..., None]), jnp.float32(0.0))
    local_sum = jnp.sum(exp_terms, axis=3)
    weights = exp_terms.astype(jnp.bfloat16)
    local_out = jnp.einsum(
        "rkgt,tkd->rkgd", weights, token_values, preferred_element_type=jnp.float32
    )

    n_blocks = n_page * n_yh
    block_rows = rows * own_heads
    out_blocks = local_out.reshape(n_yh, rows, n_page, own_heads, HD).transpose(2, 0, 1, 3, 4)
    out_blocks = out_blocks.reshape(n_blocks, block_rows, HD)
    max_blocks = local_max.reshape(n_yh, rows, n_page, own_heads).transpose(2, 0, 1, 3)
    sum_blocks = local_sum.reshape(n_yh, rows, n_page, own_heads).transpose(2, 0, 1, 3)
    stat_cols = -(-2 * block_rows // HD) * HD
    stats = jnp.concatenate(
        [
            max_blocks.reshape(n_blocks, block_rows),
            sum_blocks.reshape(n_blocks, block_rows),
            jnp.zeros((n_blocks, stat_cols - 2 * block_rows), jnp.float32),
        ],
        axis=1,
    )
    payload = jnp.concatenate([out_blocks, stats.reshape(n_blocks, -1, HD)], axis=1)
    arrived = lax.all_to_all(payload, ("page", "yh"), 0, 0, tiled=True)

    part_out = arrived[:, :block_rows, :]
    part_stats = arrived[:, block_rows:, :].reshape(n_blocks, stat_cols)
    part_max = part_stats[:, :block_rows]
    part_sum = part_stats[:, block_rows : 2 * block_rows]
    joint_max = jnp.max(part_max, axis=0)
    factor = jnp.exp(part_max - joint_max[None, :])
    joint_sum = jnp.sum(part_sum * factor, axis=0)
    joint_out = jnp.sum(part_out * factor[..., None], axis=0)
    result = joint_out / joint_sum[:, None]
    return result.reshape(rows, own_heads * HD).astype(jnp.bfloat16)


def solution(mesh):
    n_page, n_req = mesh.devices.shape
    n_yh = 2 if n_req % 2 == 0 else 1
    split = Mesh(mesh.devices.reshape(n_page, n_yh, n_req // n_yh), ("page", "yh", "xc"))
    req = ("yh", "xc")
    return jax.shard_map(
        body,
        mesh=split,
        in_specs=(
            P(req, None),
            P(("page",) + req, None, None),
            P(("page",) + req, None, None),
            P(req, None),
            P(req),
        ),
        out_specs=P(req, "page"),
        check_vma=False,
    )
```

```python
import math

import jax
import jax.numpy as jnp
from jax import lax
from jax.sharding import Mesh
from jax.sharding import PartitionSpec as P

H = 64
KVH = 8
HD = 128
LANES = 128


def split_pair(value):
    high = lax.reduce_precision(value, exponent_bits=8, mantissa_bits=7)
    low = lax.reduce_precision(value - high, exponent_bits=8, mantissa_bits=7)
    return high, low


def body(queries, key_pool, value_pool, page_table, page_count):
    n_page = lax.axis_size("page")
    n_yh = lax.axis_size("yh")
    n_xc = lax.axis_size("xc")
    page_index = lax.axis_index("page")
    yh_index = lax.axis_index("yh")
    pages_held = key_pool.shape[0]
    page_len = key_pool.shape[1]
    per_kv = H // KVH
    own_heads = H // n_page
    rows = queries.shape[0]
    score_scale = 1.0 / math.sqrt(HD)

    row_pages = n_yh * n_xc * pages_held
    row_ids = page_index * row_pages + jnp.arange(row_pages, dtype=jnp.int32)
    slot_live = jnp.arange(page_table.shape[1], dtype=jnp.int32)[None, :] < page_count[:, None]
    row_hit = jnp.any(
        (page_table[:, :, None] == row_ids[None, None, :]) & slot_live[:, :, None], axis=1
    )
    mask_cols = -(-row_pages // LANES) * LANES
    row_hit = jnp.pad(row_hit.astype(queries.dtype), ((0, 0), (0, mask_cols - row_pages)))
    packed = jnp.concatenate([queries, row_hit], axis=1)

    all_packed = lax.all_gather(packed, "yh", tiled=True)
    keys = lax.all_gather(key_pool, "xc", tiled=True)
    values = lax.all_gather(value_pool, "xc", tiled=True)

    req_rows = all_packed.shape[0]
    all_q = all_packed[:, : H * HD]
    held = n_xc * pages_held
    page_hit = lax.dynamic_slice_in_dim(all_packed, H * HD + yh_index * held, held, 1) > 0.5
    token_hit = jnp.repeat(page_hit, page_len, axis=1)[:, None, None, :]

    grouped = all_q.reshape(req_rows, KVH, per_kv, HD)
    token_keys = keys.reshape(-1, KVH, HD)
    token_values = values.reshape(-1, KVH, HD)
    scores = (
        jnp.einsum("rkgd,tkd->rkgt", grouped, token_keys, preferred_element_type=jnp.float32)
        * score_scale
    )
    scores = jnp.where(token_hit, scores, jnp.float32(-1e30))
    max_hi, max_lo = split_pair(jnp.max(scores, axis=3))
    local_max = max_hi + max_lo
    exp_terms = jnp.where(token_hit, jnp.exp(scores - local_max[..., None]), jnp.float32(0.0))
    local_sum = jnp.sum(exp_terms, axis=3)
    weights = exp_terms.astype(jnp.bfloat16)
    local_out = jnp.einsum(
        "rkgt,tkd->rkgd", weights, token_values, preferred_element_type=jnp.float32
    )

    n_blocks = n_page * n_yh
    block_rows = rows * own_heads
    out_blocks = local_out.astype(jnp.bfloat16)
    out_blocks = out_blocks.reshape(n_yh, rows, n_page, own_heads, HD).transpose(2, 0, 1, 3, 4)
    out_blocks = out_blocks.reshape(n_blocks, block_rows, HD)
    sum_hi, sum_lo = split_pair(local_sum)

    def to_blocks(stat):
        stat = stat.astype(jnp.bfloat16).reshape(n_yh, rows, n_page, own_heads).transpose(2, 0, 1, 3)
        return stat.reshape(n_blocks, block_rows)

    stat_cols = -(-4 * block_rows // HD) * HD
    stats = jnp.concatenate(
        [to_blocks(max_hi), to_blocks(max_lo), to_blocks(sum_hi), to_blocks(sum_lo)]
        + [jnp.zeros((n_blocks, stat_cols - 4 * block_rows), jnp.bfloat16)],
        axis=1,
    )
    payload = jnp.concatenate([out_blocks, stats.reshape(n_blocks, -1, HD)], axis=1)
    arrived = lax.all_to_all(payload, ("page", "yh"), 0, 0, tiled=True)

    part_out = arrived[:, :block_rows, :].astype(jnp.float32)
    part_stats = arrived[:, block_rows:, :].reshape(n_blocks, stat_cols).astype(jnp.float32)
    part_max = part_stats[:, :block_rows] + part_stats[:, block_rows : 2 * block_rows]
    part_sum = part_stats[:, 2 * block_rows : 3 * block_rows] + part_stats[:, 3 * block_rows : 4 * block_rows]
    joint_max = jnp.max(part_max, axis=0)
    factor = jnp.exp(part_max - joint_max[None, :])
    joint_sum = jnp.sum(part_sum * factor, axis=0)
    joint_out = jnp.sum(part_out * factor[..., None], axis=0)
    result = joint_out / joint_sum[:, None]
    return result.reshape(rows, own_heads * HD).astype(jnp.bfloat16)


def solution(mesh):
    n_page, n_req = mesh.devices.shape
    n_yh = 2 if n_req % 2 == 0 else 1
    split = Mesh(mesh.devices.reshape(n_page, n_yh, n_req // n_yh), ("page", "yh", "xc"))
    req = ("yh", "xc")
    return jax.shard_map(
        body,
        mesh=split,
        in_specs=(
            P(req, None),
            P(("page",) + req, None, None),
            P(("page",) + req, None, None),
            P(req, None),
            P(req),
        ),
        out_specs=P(req, "page"),
        check_vma=False,
    )
```

```python
import math

import jax
import jax.numpy as jnp
from jax import lax
from jax.sharding import Mesh
from jax.sharding import PartitionSpec as P

H = 64
KVH = 8
HD = 128
LANES = 128


def split_pair(value):
    high = lax.reduce_precision(value, exponent_bits=8, mantissa_bits=7)
    low = lax.reduce_precision(value - high, exponent_bits=8, mantissa_bits=7)
    return high, low


def body(queries, key_pool, value_pool, page_table, page_count):
    n_page = lax.axis_size("page")
    n_yh = lax.axis_size("yh")
    n_xc = lax.axis_size("xc")
    page_index = lax.axis_index("page")
    yh_index = lax.axis_index("yh")
    pages_held = key_pool.shape[0]
    page_len = key_pool.shape[1]
    per_kv = H // KVH
    own_heads = H // n_page
    rows = queries.shape[0]
    score_scale = 1.0 / math.sqrt(HD)

    row_pages = n_yh * n_xc * pages_held
    row_ids = page_index * row_pages + jnp.arange(row_pages, dtype=jnp.int32)
    slot_live = jnp.arange(page_table.shape[1], dtype=jnp.int32)[None, :] < page_count[:, None]
    row_hit = jnp.any(
        (page_table[:, :, None] == row_ids[None, None, :]) & slot_live[:, :, None], axis=1
    )
    mask_cols = -(-row_pages // LANES) * LANES
    row_hit = jnp.pad(row_hit.astype(queries.dtype), ((0, 0), (0, mask_cols - row_pages)))
    packed = jnp.concatenate([queries, row_hit], axis=1)

    all_packed = lax.all_gather(packed, "yh", tiled=True)
    keys = lax.all_gather(key_pool, "xc", tiled=True)
    values = lax.all_to_all(
        jnp.broadcast_to(value_pool[None], (n_xc,) + value_pool.shape).reshape(
            (n_xc * pages_held,) + value_pool.shape[1:]
        ),
        "xc",
        0,
        0,
        tiled=True,
    )

    req_rows = all_packed.shape[0]
    all_q = all_packed[:, : H * HD]
    held = n_xc * pages_held
    page_hit = lax.dynamic_slice_in_dim(all_packed, H * HD + yh_index * held, held, 1) > 0.5
    token_hit = jnp.repeat(page_hit, page_len, axis=1)[:, None, None, :]

    grouped = all_q.reshape(req_rows, KVH, per_kv, HD)
    token_keys = keys.reshape(-1, KVH, HD)
    token_values = values.reshape(-1, KVH, HD)
    scores = (
        jnp.einsum("rkgd,tkd->rkgt", grouped, token_keys, preferred_element_type=jnp.float32)
        * score_scale
    )
    scores = jnp.where(token_hit, scores, jnp.float32(-1e30))
    max_hi, max_lo = split_pair(jnp.max(scores, axis=3))
    local_max = max_hi + max_lo
    exp_terms = jnp.where(token_hit, jnp.exp(scores - local_max[..., None]), jnp.float32(0.0))
    local_sum = jnp.sum(exp_terms, axis=3)
    weights = exp_terms.astype(jnp.bfloat16)
    local_out = jnp.einsum(
        "rkgt,tkd->rkgd", weights, token_values, preferred_element_type=jnp.float32
    )

    n_blocks = n_page * n_yh
    block_rows = rows * own_heads
    out_blocks = local_out.astype(jnp.bfloat16)
    out_blocks = out_blocks.reshape(n_yh, rows, n_page, own_heads, HD).transpose(2, 0, 1, 3, 4)
    out_blocks = out_blocks.reshape(n_blocks, block_rows, HD)
    sum_hi, sum_lo = split_pair(local_sum)

    def to_blocks(stat):
        stat = stat.astype(jnp.bfloat16).reshape(n_yh, rows, n_page, own_heads).transpose(2, 0, 1, 3)
        return stat.reshape(n_blocks, block_rows)

    stat_cols = -(-4 * block_rows // HD) * HD
    stats = jnp.concatenate(
        [to_blocks(max_hi), to_blocks(max_lo), to_blocks(sum_hi), to_blocks(sum_lo)]
        + [jnp.zeros((n_blocks, stat_cols - 4 * block_rows), jnp.bfloat16)],
        axis=1,
    )
    payload = jnp.concatenate([out_blocks, stats.reshape(n_blocks, -1, HD)], axis=1)
    arrived = lax.all_to_all(payload, ("page", "yh"), 0, 0, tiled=True)

    part_out = arrived[:, :block_rows, :].astype(jnp.float32)
    part_stats = arrived[:, block_rows:, :].reshape(n_blocks, stat_cols).astype(jnp.float32)
    part_max = part_stats[:, :block_rows] + part_stats[:, block_rows : 2 * block_rows]
    part_sum = part_stats[:, 2 * block_rows : 3 * block_rows] + part_stats[:, 3 * block_rows : 4 * block_rows]
    joint_max = jnp.max(part_max, axis=0)
    factor = jnp.exp(part_max - joint_max[None, :])
    joint_sum = jnp.sum(part_sum * factor, axis=0)
    joint_out = jnp.sum(part_out * factor[..., None], axis=0)
    result = joint_out / joint_sum[:, None]
    return result.reshape(rows, own_heads * HD).astype(jnp.bfloat16)


def solution(mesh):
    n_page, n_req = mesh.devices.shape
    n_yh = 2 if n_req % 2 == 0 else 1
    split = Mesh(mesh.devices.reshape(n_page, n_yh, n_req // n_yh), ("page", "yh", "xc"))
    req = ("yh", "xc")
    return jax.shard_map(
        body,
        mesh=split,
        in_specs=(
            P(req, None),
            P(("page",) + req, None, None),
            P(("page",) + req, None, None),
            P(req, None),
            P(req),
        ),
        out_specs=P(req, "page"),
        check_vma=False,
    )
```

```python
import math

import jax
import jax.numpy as jnp
from jax import lax
from jax.experimental import pallas as pl
from jax.experimental.pallas import tpu as pltpu
from jax.sharding import Mesh
from jax.sharding import PartitionSpec as P

H = 64
KVH = 8
HD = 128
LANES = 128


def split_pair(value):
    high = lax.reduce_precision(value, exponent_bits=8, mantissa_bits=7)
    low = lax.reduce_precision(value - high, exponent_bits=8, mantissa_bits=7)
    return high, low


def attend_kernel(q_ref, k_ref, v_ref, hit_ref, out_ref, stat_ref):
    pages, page_len, _ = k_ref.shape
    q = q_ref[0]
    keys = k_ref[...].reshape(pages * page_len, HD)
    values = v_ref[...].reshape(pages * page_len, HD)
    scores = lax.dot_general(
        q, keys, (((1,), (1,)), ((), ())), preferred_element_type=jnp.float32
    ) * (1.0 / math.sqrt(HD))
    req_rows = hit_ref.shape[0]
    groups = q.shape[0] // req_rows
    hit = jnp.concatenate([hit_ref[...]] * groups, axis=0) > 0.5
    scores = jnp.where(hit, scores, jnp.float32(-1e30))
    top = jnp.max(scores, axis=1, keepdims=True)
    high = top.astype(jnp.bfloat16).astype(jnp.float32)
    low = (top - high).astype(jnp.bfloat16).astype(jnp.float32)
    shift = high + low
    terms = jnp.where(hit, jnp.exp(scores - shift), jnp.float32(0.0))
    total = jnp.sum(terms, axis=1, keepdims=True)
    out_ref[0] = jnp.dot(
        terms.astype(jnp.bfloat16), values, preferred_element_type=jnp.float32
    )
    lane = lax.broadcasted_iota(jnp.int32, (q.shape[0], LANES), 1)
    stat_ref[0] = jnp.where(
        lane == 0, high, jnp.where(lane == 1, low, jnp.where(lane == 2, total, 0.0))
    )


def attend(grouped_q, keys, values, token_hit):
    kv_heads, q_rows, _ = grouped_q.shape
    pages, page_len, _ = keys.shape
    tokens = pages * page_len
    return pl.pallas_call(
        attend_kernel,
        grid=(kv_heads,),
        in_specs=[
            pl.BlockSpec((1, q_rows, HD), lambda k: (k, 0, 0)),
            pl.BlockSpec((pages, page_len, HD), lambda k: (0, 0, k)),
            pl.BlockSpec((pages, page_len, HD), lambda k: (0, 0, k)),
            pl.BlockSpec(token_hit.shape, lambda k: (0, 0)),
        ],
        out_specs=[
            pl.BlockSpec((1, q_rows, HD), lambda k: (k, 0, 0)),
            pl.BlockSpec((1, q_rows, LANES), lambda k: (k, 0, 0)),
        ],
        out_shape=[
            jax.ShapeDtypeStruct((kv_heads, q_rows, HD), jnp.float32),
            jax.ShapeDtypeStruct((kv_heads, q_rows, LANES), jnp.float32),
        ],
        cost_estimate=pl.CostEstimate(
            flops=4 * kv_heads * q_rows * tokens * HD,
            transcendentals=kv_heads * q_rows * tokens,
            bytes_accessed=2 * (grouped_q.size + keys.size + values.size) + 4 * 2 * kv_heads * q_rows * HD,
        ),
    )(grouped_q, keys, values, token_hit)


def body(queries, key_pool, value_pool, page_table, page_count):
    n_page = lax.axis_size("page")
    n_yh = lax.axis_size("yh")
    n_xc = lax.axis_size("xc")
    page_index = lax.axis_index("page")
    yh_index = lax.axis_index("yh")
    pages_held = key_pool.shape[0]
    page_len = key_pool.shape[1]
    per_kv = H // KVH
    own_heads = H // n_page
    rows = queries.shape[0]
    score_scale = 1.0 / math.sqrt(HD)

    row_pages = n_yh * n_xc * pages_held
    row_ids = page_index * row_pages + jnp.arange(row_pages, dtype=jnp.int32)
    slot_live = jnp.arange(page_table.shape[1], dtype=jnp.int32)[None, :] < page_count[:, None]
    row_hit = jnp.any(
        (page_table[:, :, None] == row_ids[None, None, :]) & slot_live[:, :, None], axis=1
    )
    mask_cols = -(-row_pages // LANES) * LANES
    row_hit = jnp.pad(row_hit.astype(queries.dtype), ((0, 0), (0, mask_cols - row_pages)))
    packed = jnp.concatenate([queries, row_hit], axis=1)

    all_packed = lax.all_gather(packed, "yh", tiled=True)
    keys = lax.all_gather(key_pool, "xc", tiled=True)
    values = lax.all_to_all(
        jnp.broadcast_to(value_pool[None], (n_xc,) + value_pool.shape).reshape(
            (n_xc * pages_held,) + value_pool.shape[1:]
        ),
        "xc",
        0,
        0,
        tiled=True,
    )

    req_rows = all_packed.shape[0]
    all_q = all_packed[:, : H * HD]
    held = n_xc * pages_held
    page_hit = lax.dynamic_slice_in_dim(all_packed, H * HD + yh_index * held, held, 1) > 0.5
    token_hit = jnp.repeat(page_hit, page_len, axis=1).astype(jnp.float32)

    grouped = all_q.reshape(req_rows, KVH, per_kv, HD).transpose(1, 2, 0, 3)
    grouped = grouped.reshape(KVH, per_kv * req_rows, HD)
    out_k, stat_k = attend(grouped, keys, values, token_hit)
    local_out = out_k.reshape(KVH, per_kv, req_rows, HD).transpose(2, 0, 1, 3)
    stat_k = stat_k.reshape(KVH, per_kv, req_rows, LANES).transpose(2, 0, 1, 3)
    max_hi = stat_k[..., 0]
    max_lo = stat_k[..., 1]
    local_sum = stat_k[..., 2]

    n_blocks = n_page * n_yh
    block_rows = rows * own_heads
    out_blocks = local_out.astype(jnp.bfloat16)
    out_blocks = out_blocks.reshape(n_yh, rows, n_page, own_heads, HD).transpose(2, 0, 1, 3, 4)
    out_blocks = out_blocks.reshape(n_blocks, block_rows, HD)
    sum_hi, sum_lo = split_pair(local_sum)

    def to_blocks(stat):
        stat = stat.astype(jnp.bfloat16).reshape(n_yh, rows, n_page, own_heads).transpose(2, 0, 1, 3)
        return stat.reshape(n_blocks, block_rows)

    stat_cols = -(-4 * block_rows // HD) * HD
    stats = jnp.concatenate(
        [to_blocks(max_hi), to_blocks(max_lo), to_blocks(sum_hi), to_blocks(sum_lo)]
        + [jnp.zeros((n_blocks, stat_cols - 4 * block_rows), jnp.bfloat16)],
        axis=1,
    )
    payload = jnp.concatenate([out_blocks, stats.reshape(n_blocks, -1, HD)], axis=1)
    arrived = lax.all_to_all(payload, ("page", "yh"), 0, 0, tiled=True)

    part_out = arrived[:, :block_rows, :].astype(jnp.float32)
    part_stats = arrived[:, block_rows:, :].reshape(n_blocks, stat_cols).astype(jnp.float32)
    part_max = part_stats[:, :block_rows] + part_stats[:, block_rows : 2 * block_rows]
    part_sum = part_stats[:, 2 * block_rows : 3 * block_rows] + part_stats[:, 3 * block_rows : 4 * block_rows]
    joint_max = jnp.max(part_max, axis=0)
    factor = jnp.exp(part_max - joint_max[None, :])
    joint_sum = jnp.sum(part_sum * factor, axis=0)
    joint_out = jnp.sum(part_out * factor[..., None], axis=0)
    result = joint_out / joint_sum[:, None]
    return result.reshape(rows, own_heads * HD).astype(jnp.bfloat16)


def solution(mesh):
    n_page, n_req = mesh.devices.shape
    n_yh = 2 if n_req % 2 == 0 else 1
    split = Mesh(mesh.devices.reshape(n_page, n_yh, n_req // n_yh), ("page", "yh", "xc"))
    req = ("yh", "xc")
    return jax.shard_map(
        body,
        mesh=split,
        in_specs=(
            P(req, None),
            P(("page",) + req, None, None),
            P(("page",) + req, None, None),
            P(req, None),
            P(req),
        ),
        out_specs=P(req, "page"),
        check_vma=False,
    )
```

```python
import functools
import math

import jax
import jax.numpy as jnp
from jax import lax
from jax.experimental import pallas as pl
from jax.experimental.pallas import tpu as pltpu
from jax.sharding import Mesh
from jax.sharding import PartitionSpec as P

H = 64
KVH = 8
HD = 128
LANES = 128
STAT_ROWS = 8


def split_pair(value):
    high = lax.reduce_precision(value, exponent_bits=8, mantissa_bits=7)
    low = lax.reduce_precision(value - high, exponent_bits=8, mantissa_bits=7)
    return high, low


def attend_kernel(rows, own_heads, q_ref, k_ref, v_ref, hit_ref, out_ref, stat_ref):
    pages, page_len, _ = k_ref.shape
    q = q_ref[0]
    keys = k_ref[...].reshape(pages * page_len, HD)
    values = v_ref[...].reshape(pages * page_len, HD)
    scores = lax.dot_general(
        q, keys, (((1,), (1,)), ((), ())), preferred_element_type=jnp.float32
    ) * (1.0 / math.sqrt(HD))
    req_rows = hit_ref.shape[0]
    groups = q.shape[0] // req_rows
    halves = req_rows // rows
    hit = jnp.concatenate([hit_ref[...]] * groups, axis=0) > 0.5
    scores = jnp.where(hit, scores, jnp.float32(-1e30))
    top = jnp.max(scores, axis=1, keepdims=True)
    high = top.astype(jnp.bfloat16).astype(jnp.float32)
    low = (top - high).astype(jnp.bfloat16).astype(jnp.float32)
    shift = high + low
    terms = jnp.where(hit, jnp.exp(scores - shift), jnp.float32(0.0))
    total = jnp.sum(terms, axis=1, keepdims=True)
    mixed = jnp.dot(
        terms.astype(jnp.bfloat16), values, preferred_element_type=jnp.float32
    ).astype(jnp.bfloat16)
    for g in range(groups):
        for y in range(halves):
            first = g * req_rows + y * rows
            block = (g // own_heads) * halves + y
            row = (g % own_heads) * rows
            out_ref[block, row : row + rows, :] = mixed[first : first + rows, :]
    lane = lax.broadcasted_iota(jnp.int32, (q.shape[0], LANES), 1)
    stat_tile = jnp.where(
        lane == 0, high, jnp.where(lane == 1, low, jnp.where(lane == 2, total, 0.0))
    )
    stat_ref[0] = jnp.transpose(stat_tile)[: stat_ref.shape[1], :]


def attend(grouped_q, keys, values, token_hit, rows, own_heads):
    kv_heads, q_rows, _ = grouped_q.shape
    pages, page_len, _ = keys.shape
    tokens = pages * page_len
    req_rows = token_hit.shape[0]
    groups = q_rows // req_rows
    per_head_blocks = groups // own_heads * (req_rows // rows)
    block_rows = own_heads * rows
    return pl.pallas_call(
        functools.partial(attend_kernel, rows, own_heads),
        grid=(kv_heads,),
        in_specs=[
            pl.BlockSpec((1, q_rows, HD), lambda k: (k, 0, 0)),
            pl.BlockSpec((pages, page_len, HD), lambda k: (0, 0, k)),
            pl.BlockSpec((pages, page_len, HD), lambda k: (0, 0, k)),
            pl.BlockSpec(token_hit.shape, lambda k: (0, 0)),
        ],
        out_specs=[
            pl.BlockSpec((per_head_blocks, block_rows, HD), lambda k: (k, 0, 0)),
            pl.BlockSpec((1, STAT_ROWS, q_rows), lambda k: (k, 0, 0)),
        ],
        out_shape=[
            jax.ShapeDtypeStruct((kv_heads * per_head_blocks, block_rows, HD), jnp.bfloat16),
            jax.ShapeDtypeStruct((kv_heads, STAT_ROWS, q_rows), jnp.float32),
        ],
        cost_estimate=pl.CostEstimate(
            flops=4 * kv_heads * q_rows * tokens * HD,
            transcendentals=kv_heads * q_rows * tokens,
            bytes_accessed=2 * (grouped_q.size + keys.size + values.size) + 6 * kv_heads * q_rows * HD,
        ),
    )(grouped_q, keys, values, token_hit)

def body(queries, key_pool, value_pool, page_table, page_count):
    n_page = lax.axis_size("page")
    n_yh = lax.axis_size("yh")
    n_xc = lax.axis_size("xc")
    page_index = lax.axis_index("page")
    yh_index = lax.axis_index("yh")
    pages_held = key_pool.shape[0]
    page_len = key_pool.shape[1]
    per_kv = H // KVH
    own_heads = H // n_page
    rows = queries.shape[0]
    score_scale = 1.0 / math.sqrt(HD)

    row_pages = n_yh * n_xc * pages_held
    row_ids = page_index * row_pages + jnp.arange(row_pages, dtype=jnp.int32)
    slot_live = jnp.arange(page_table.shape[1], dtype=jnp.int32)[None, :] < page_count[:, None]
    row_hit = jnp.any(
        (page_table[:, :, None] == row_ids[None, None, :]) & slot_live[:, :, None], axis=1
    )
    mask_cols = -(-row_pages // LANES) * LANES
    row_hit = jnp.pad(row_hit.astype(queries.dtype), ((0, 0), (0, mask_cols - row_pages)))
    packed = jnp.concatenate([queries, row_hit], axis=1)

    all_packed = lax.all_gather(packed, "yh", tiled=True)
    keys = lax.all_gather(key_pool, "xc", tiled=True)
    values = lax.all_to_all(
        jnp.broadcast_to(value_pool[None], (n_xc,) + value_pool.shape).reshape(
            (n_xc * pages_held,) + value_pool.shape[1:]
        ),
        "xc",
        0,
        0,
        tiled=True,
    )

    req_rows = all_packed.shape[0]
    all_q = all_packed[:, : H * HD]
    held = n_xc * pages_held
    page_hit = lax.dynamic_slice_in_dim(all_packed, H * HD + yh_index * held, held, 1) > 0.5
    token_hit = jnp.repeat(page_hit, page_len, axis=1).astype(jnp.float32)

    grouped = all_q.reshape(req_rows, KVH, per_kv, HD).transpose(1, 2, 0, 3)
    grouped = grouped.reshape(KVH, per_kv * req_rows, HD)
    n_blocks = n_page * n_yh
    block_rows = rows * own_heads
    out_blocks, stat_k = attend(grouped, keys, values, token_hit, rows, own_heads)
    stat_k = stat_k[:, :3, :].reshape(KVH, 3, per_kv // own_heads, own_heads, n_yh, rows)
    stat_k = stat_k.transpose(1, 0, 2, 4, 3, 5).reshape(3, n_blocks, block_rows)
    max_hi = stat_k[0]
    max_lo = stat_k[1]
    sum_hi, sum_lo = split_pair(stat_k[2])
    stat_cols = -(-4 * block_rows // HD) * HD
    stats = jnp.concatenate(
        [max_hi, max_lo, sum_hi, sum_lo]
        + [jnp.zeros((n_blocks, stat_cols - 4 * block_rows), jnp.float32)],
        axis=1,
    ).astype(jnp.bfloat16)
    payload = jnp.concatenate([out_blocks, stats.reshape(n_blocks, -1, HD)], axis=1)
    arrived = lax.all_to_all(payload, ("page", "yh"), 0, 0, tiled=True)

    part_out = arrived[:, :block_rows, :].astype(jnp.float32)
    part_stats = arrived[:, block_rows:, :].reshape(n_blocks, stat_cols).astype(jnp.float32)
    part_max = part_stats[:, :block_rows] + part_stats[:, block_rows : 2 * block_rows]
    part_sum = part_stats[:, 2 * block_rows : 3 * block_rows] + part_stats[:, 3 * block_rows : 4 * block_rows]
    joint_max = jnp.max(part_max, axis=0)
    factor = jnp.exp(part_max - joint_max[None, :])
    joint_sum = jnp.sum(part_sum * factor, axis=0)
    joint_out = jnp.sum(part_out * factor[..., None], axis=0)
    result = (joint_out / joint_sum[:, None]).reshape(own_heads, rows, HD).transpose(1, 0, 2)
    return result.reshape(rows, own_heads * HD).astype(jnp.bfloat16)


def solution(mesh):
    n_page, n_req = mesh.devices.shape
    n_yh = 2 if n_req % 2 == 0 else 1
    split = Mesh(mesh.devices.reshape(n_page, n_yh, n_req // n_yh), ("page", "yh", "xc"))
    req = ("yh", "xc")
    return jax.shard_map(
        body,
        mesh=split,
        in_specs=(
            P(req, None),
            P(("page",) + req, None, None),
            P(("page",) + req, None, None),
            P(req, None),
            P(req),
        ),
        out_specs=P(req, "page"),
        check_vma=False,
    )
```

```python
import functools
import math

import jax
import jax.numpy as jnp
from jax import lax
from jax.experimental import pallas as pl
from jax.experimental.pallas import tpu as pltpu
from jax.sharding import Mesh
from jax.sharding import PartitionSpec as P

H = 64
KVH = 8
HD = 128
LANES = 128
STAT_ROWS = 8


def split_pair(value):
    high = lax.reduce_precision(value, exponent_bits=8, mantissa_bits=7)
    low = lax.reduce_precision(value - high, exponent_bits=8, mantissa_bits=7)
    return high, low


def attend_kernel(rows, own_heads, q_ref, k_ref, v_ref, hit_ref, out_ref, stat_ref):
    pages, page_len, _ = k_ref.shape
    q = q_ref[0]
    keys = k_ref[...].reshape(pages * page_len, HD)
    values = v_ref[...].reshape(pages * page_len, HD)
    scores = lax.dot_general(
        q, keys, (((1,), (1,)), ((), ())), preferred_element_type=jnp.float32
    ) * (1.0 / math.sqrt(HD))
    req_rows = hit_ref.shape[0]
    groups = q.shape[0] // req_rows
    halves = req_rows // rows
    hit = jnp.concatenate([hit_ref[...]] * groups, axis=0) > 0.5
    scores = jnp.where(hit, scores, jnp.float32(-1e30))
    top = jnp.max(scores, axis=1, keepdims=True)
    high = top.astype(jnp.bfloat16).astype(jnp.float32)
    low = (top - high).astype(jnp.bfloat16).astype(jnp.float32)
    shift = high + low
    terms = jnp.where(hit, jnp.exp(scores - shift), jnp.float32(0.0))
    total = jnp.sum(terms, axis=1, keepdims=True)
    mixed = jnp.dot(
        terms.astype(jnp.bfloat16), values, preferred_element_type=jnp.float32
    ).astype(jnp.bfloat16)
    for g in range(groups):
        for y in range(halves):
            first = g * req_rows + y * rows
            block = (g // own_heads) * halves + y
            row = (g % own_heads) * rows
            out_ref[block, row : row + rows, :] = mixed[first : first + rows, :]
    lane = lax.broadcasted_iota(jnp.int32, (q.shape[0], LANES), 1)
    stat_tile = jnp.where(
        lane == 0, high, jnp.where(lane == 1, low, jnp.where(lane == 2, total, 0.0))
    )
    stat_ref[0] = jnp.transpose(stat_tile)[: stat_ref.shape[1], :]


def attend(grouped_q, keys, values, token_hit, rows, own_heads):
    kv_heads, q_rows, _ = grouped_q.shape
    pages, page_len, _ = keys.shape
    tokens = pages * page_len
    req_rows = token_hit.shape[0]
    groups = q_rows // req_rows
    per_head_blocks = groups // own_heads * (req_rows // rows)
    block_rows = own_heads * rows
    return pl.pallas_call(
        functools.partial(attend_kernel, rows, own_heads),
        grid=(kv_heads,),
        in_specs=[
            pl.BlockSpec((1, q_rows, HD), lambda k: (k, 0, 0)),
            pl.BlockSpec((pages, page_len, HD), lambda k: (0, 0, k)),
            pl.BlockSpec((pages, page_len, HD), lambda k: (0, 0, k)),
            pl.BlockSpec(token_hit.shape, lambda k: (0, 0)),
        ],
        out_specs=[
            pl.BlockSpec((per_head_blocks, block_rows, HD), lambda k: (k, 0, 0)),
            pl.BlockSpec((1, STAT_ROWS, q_rows), lambda k: (k, 0, 0)),
        ],
        out_shape=[
            jax.ShapeDtypeStruct((kv_heads * per_head_blocks, block_rows, HD), jnp.bfloat16),
            jax.ShapeDtypeStruct((kv_heads, STAT_ROWS, q_rows), jnp.float32),
        ],
        cost_estimate=pl.CostEstimate(
            flops=4 * kv_heads * q_rows * tokens * HD,
            transcendentals=kv_heads * q_rows * tokens,
            bytes_accessed=2 * (grouped_q.size + keys.size + values.size) + 6 * kv_heads * q_rows * HD,
        ),
    )(grouped_q, keys, values, token_hit)

def body(queries, key_pool, value_pool, page_table, page_count):
    n_page = lax.axis_size("page")
    n_yh = lax.axis_size("yh")
    n_xc = lax.axis_size("xc")
    page_index = lax.axis_index("page")
    yh_index = lax.axis_index("yh")
    pages_held = key_pool.shape[0]
    page_len = key_pool.shape[1]
    per_kv = H // KVH
    own_heads = H // n_page
    rows = queries.shape[0]
    score_scale = 1.0 / math.sqrt(HD)

    row_pages = n_yh * n_xc * pages_held
    row_ids = page_index * row_pages + jnp.arange(row_pages, dtype=jnp.int32)
    slot_live = jnp.arange(page_table.shape[1], dtype=jnp.int32)[None, :] < page_count[:, None]
    row_hit = jnp.any(
        (page_table[:, :, None] == row_ids[None, None, :]) & slot_live[:, :, None], axis=1
    )
    mask_cols = -(-row_pages // LANES) * LANES
    row_hit = jnp.pad(row_hit.astype(queries.dtype), ((0, 0), (0, mask_cols - row_pages)))
    packed = jnp.concatenate([queries, row_hit], axis=1)

    all_packed = lax.all_gather(packed, "yh", tiled=True)
    keys = lax.all_gather(key_pool, "xc", tiled=True)
    values = lax.all_to_all(
        jnp.broadcast_to(value_pool[None], (n_xc,) + value_pool.shape).reshape(
            (n_xc * pages_held,) + value_pool.shape[1:]
        ),
        "xc",
        0,
        0,
        tiled=True,
    )

    req_rows = all_packed.shape[0]
    all_q = all_packed[:, : H * HD]
    held = n_xc * pages_held
    page_hit = lax.dynamic_slice_in_dim(all_packed, H * HD + yh_index * held, held, 1) > 0.5
    token_hit = jnp.repeat(page_hit, page_len, axis=1).astype(jnp.float32)

    grouped = all_q.reshape(req_rows, KVH, per_kv, HD).transpose(1, 2, 0, 3)
    grouped = grouped.reshape(KVH, per_kv * req_rows, HD)
    n_blocks = n_page * n_yh
    block_rows = rows * own_heads
    out_blocks, stat_k = attend(grouped, keys, values, token_hit, rows, own_heads)
    stat_k = stat_k[:, :3, :].reshape(KVH, 3, per_kv // own_heads, own_heads, n_yh, rows)
    stat_k = stat_k.transpose(1, 0, 2, 4, 3, 5).reshape(3, n_blocks, block_rows)
    max_hi = stat_k[0]
    max_lo = stat_k[1]
    sum_hi, sum_lo = split_pair(stat_k[2])
    stat_cols = -(-4 * block_rows // HD) * HD
    stats = jnp.concatenate(
        [max_hi, max_lo, sum_hi, sum_lo]
        + [jnp.zeros((n_blocks, stat_cols - 4 * block_rows), jnp.float32)],
        axis=1,
    ).astype(jnp.bfloat16)
    payload = jnp.concatenate([out_blocks.reshape(n_blocks, block_rows * HD), stats], axis=1)
    arrived = lax.all_to_all(payload, ("page", "yh"), 0, 0, tiled=True)

    part_out = arrived[:, : block_rows * HD].reshape(n_blocks, block_rows, HD).astype(jnp.float32)
    part_stats = arrived[:, block_rows * HD :].astype(jnp.float32)
    part_max = part_stats[:, :block_rows] + part_stats[:, block_rows : 2 * block_rows]
    part_sum = part_stats[:, 2 * block_rows : 3 * block_rows] + part_stats[:, 3 * block_rows : 4 * block_rows]
    joint_max = jnp.max(part_max, axis=0)
    factor = jnp.exp(part_max - joint_max[None, :])
    joint_sum = jnp.sum(part_sum * factor, axis=0)
    joint_out = jnp.sum(part_out * factor[..., None], axis=0)
    result = (joint_out / joint_sum[:, None]).reshape(own_heads, rows, HD).transpose(1, 0, 2)
    return result.reshape(rows, own_heads * HD).astype(jnp.bfloat16)


def solution(mesh):
    n_page, n_req = mesh.devices.shape
    n_yh = 2 if n_req % 2 == 0 else 1
    split = Mesh(mesh.devices.reshape(n_page, n_yh, n_req // n_yh), ("page", "yh", "xc"))
    req = ("yh", "xc")
    return jax.shard_map(
        body,
        mesh=split,
        in_specs=(
            P(req, None),
            P(("page",) + req, None, None),
            P(("page",) + req, None, None),
            P(req, None),
            P(req),
        ),
        out_specs=P(req, "page"),
        check_vma=False,
    )
```

```python
import functools
import math

import jax
import jax.numpy as jnp
from jax import lax
from jax.experimental import pallas as pl
from jax.experimental.pallas import tpu as pltpu
from jax.sharding import Mesh
from jax.sharding import PartitionSpec as P

H = 64
KVH = 8
HD = 128
LANES = 128
STAT_ROWS = 8


def split_pair(value):
    high = lax.reduce_precision(value, exponent_bits=8, mantissa_bits=7)
    low = lax.reduce_precision(value - high, exponent_bits=8, mantissa_bits=7)
    return high, low


def attend_kernel(rows, own_heads, q_ref, k_ref, v_ref, hit_ref, out_ref, stat_ref):
    pages, page_len, _ = k_ref.shape
    q = q_ref[0]
    keys = k_ref[...].reshape(pages * page_len, HD)
    values = v_ref[...].reshape(pages * page_len, HD)
    scores = lax.dot_general(
        q, keys, (((1,), (1,)), ((), ())), preferred_element_type=jnp.float32
    ) * (1.0 / math.sqrt(HD))
    req_rows = hit_ref.shape[0]
    groups = q.shape[0] // req_rows
    halves = req_rows // rows
    scores = (scores.reshape(groups, req_rows, -1) + hit_ref[...][None]).reshape(q.shape[0], -1)
    top = jnp.max(scores, axis=1, keepdims=True)
    high = top.astype(jnp.bfloat16).astype(jnp.float32)
    low = (top - high).astype(jnp.bfloat16).astype(jnp.float32)
    shift = high + low
    terms = jnp.exp(jnp.minimum(scores - shift, 1.0))
    total = jnp.sum(terms, axis=1, keepdims=True)
    mixed = jnp.dot(
        terms.astype(jnp.bfloat16), values, preferred_element_type=jnp.float32
    ).astype(jnp.bfloat16)
    for g in range(groups):
        for y in range(halves):
            first = g * req_rows + y * rows
            block = (g // own_heads) * halves + y
            row = (g % own_heads) * rows
            out_ref[block, row : row + rows, :] = mixed[first : first + rows, :]
    lane = lax.broadcasted_iota(jnp.int32, (q.shape[0], LANES), 1)
    stat_tile = jnp.where(
        lane == 0, high, jnp.where(lane == 1, low, jnp.where(lane == 2, total, 0.0))
    )
    stat_ref[0] = jnp.transpose(stat_tile)[: stat_ref.shape[1], :]


def attend(grouped_q, keys, values, token_hit, rows, own_heads):
    kv_heads, q_rows, _ = grouped_q.shape
    pages, page_len, _ = keys.shape
    tokens = pages * page_len
    req_rows = token_hit.shape[0]
    groups = q_rows // req_rows
    per_head_blocks = groups // own_heads * (req_rows // rows)
    block_rows = own_heads * rows
    return pl.pallas_call(
        functools.partial(attend_kernel, rows, own_heads),
        grid=(kv_heads,),
        in_specs=[
            pl.BlockSpec((1, q_rows, HD), lambda k: (k, 0, 0)),
            pl.BlockSpec((pages, page_len, HD), lambda k: (0, 0, k)),
            pl.BlockSpec((pages, page_len, HD), lambda k: (0, 0, k)),
            pl.BlockSpec(token_hit.shape, lambda k: (0, 0)),
        ],
        out_specs=[
            pl.BlockSpec((per_head_blocks, block_rows, HD), lambda k: (k, 0, 0)),
            pl.BlockSpec((1, STAT_ROWS, q_rows), lambda k: (k, 0, 0)),
        ],
        out_shape=[
            jax.ShapeDtypeStruct((kv_heads * per_head_blocks, block_rows, HD), jnp.bfloat16),
            jax.ShapeDtypeStruct((kv_heads, STAT_ROWS, q_rows), jnp.float32),
        ],
        cost_estimate=pl.CostEstimate(
            flops=4 * kv_heads * q_rows * tokens * HD,
            transcendentals=kv_heads * q_rows * tokens,
            bytes_accessed=2 * (grouped_q.size + keys.size + values.size) + 6 * kv_heads * q_rows * HD,
        ),
    )(grouped_q, keys, values, token_hit)

def body(queries, key_pool, value_pool, page_table, page_count):
    n_page = lax.axis_size("page")
    n_yh = lax.axis_size("yh")
    n_xc = lax.axis_size("xc")
    page_index = lax.axis_index("page")
    yh_index = lax.axis_index("yh")
    pages_held = key_pool.shape[0]
    page_len = key_pool.shape[1]
    per_kv = H // KVH
    own_heads = H // n_page
    rows = queries.shape[0]
    score_scale = 1.0 / math.sqrt(HD)

    row_pages = n_yh * n_xc * pages_held
    row_ids = page_index * row_pages + jnp.arange(row_pages, dtype=jnp.int32)
    slot_live = jnp.arange(page_table.shape[1], dtype=jnp.int32)[None, :] < page_count[:, None]
    row_hit = jnp.any(
        (page_table[:, :, None] == row_ids[None, None, :]) & slot_live[:, :, None], axis=1
    )
    mask_cols = -(-row_pages // LANES) * LANES
    row_hit = jnp.pad(row_hit.astype(queries.dtype), ((0, 0), (0, mask_cols - row_pages)))
    packed = jnp.concatenate([queries, row_hit], axis=1)

    all_packed = lax.all_gather(packed, "yh", tiled=True)
    keys = lax.all_gather(key_pool, "xc", tiled=True)
    values = lax.all_to_all(
        jnp.broadcast_to(value_pool[None], (n_xc,) + value_pool.shape).reshape(
            (n_xc * pages_held,) + value_pool.shape[1:]
        ),
        "xc",
        0,
        0,
        tiled=True,
    )

    req_rows = all_packed.shape[0]
    all_q = all_packed[:, : H * HD]
    held = n_xc * pages_held
    page_hit = lax.dynamic_slice_in_dim(all_packed, H * HD + yh_index * held, held, 1) > 0.5
    token_hit = jnp.where(jnp.repeat(page_hit, page_len, axis=1), jnp.float32(0.0), jnp.float32(-1e30))

    grouped = all_q.reshape(req_rows, KVH, per_kv, HD).transpose(1, 2, 0, 3)
    grouped = grouped.reshape(KVH, per_kv * req_rows, HD)
    n_blocks = n_page * n_yh
    block_rows = rows * own_heads
    out_blocks, stat_k = attend(grouped, keys, values, token_hit, rows, own_heads)
    stat_k = stat_k[:, :3, :].reshape(KVH, 3, per_kv // own_heads, own_heads, n_yh, rows)
    stat_k = stat_k.transpose(1, 0, 2, 4, 3, 5).reshape(3, n_blocks, block_rows)
    max_hi = stat_k[0]
    max_lo = stat_k[1]
    sum_hi, sum_lo = split_pair(stat_k[2])
    stat_cols = -(-4 * block_rows // HD) * HD
    stats = jnp.concatenate(
        [max_hi, max_lo, sum_hi, sum_lo]
        + [jnp.zeros((n_blocks, stat_cols - 4 * block_rows), jnp.float32)],
        axis=1,
    ).astype(jnp.bfloat16)
    payload = jnp.concatenate([out_blocks, stats.reshape(n_blocks, -1, HD)], axis=1)
    arrived = lax.all_to_all(payload, ("page", "yh"), 0, 0, tiled=True)

    part_out = arrived[:, :block_rows, :].astype(jnp.float32)
    part_stats = arrived[:, block_rows:, :].reshape(n_blocks, stat_cols).astype(jnp.float32)
    part_max = part_stats[:, :block_rows] + part_stats[:, block_rows : 2 * block_rows]
    part_sum = part_stats[:, 2 * block_rows : 3 * block_rows] + part_stats[:, 3 * block_rows : 4 * block_rows]
    joint_max = jnp.max(part_max, axis=0)
    factor = jnp.exp(part_max - joint_max[None, :])
    joint_sum = jnp.sum(part_sum * factor, axis=0)
    joint_out = jnp.sum(part_out * factor[..., None], axis=0)
    result = (joint_out / joint_sum[:, None]).reshape(own_heads, rows, HD).transpose(1, 0, 2)
    return result.reshape(rows, own_heads * HD).astype(jnp.bfloat16)


def solution(mesh):
    n_page, n_req = mesh.devices.shape
    n_yh = 2 if n_req % 2 == 0 else 1
    split = Mesh(mesh.devices.reshape(n_page, n_yh, n_req // n_yh), ("page", "yh", "xc"))
    req = ("yh", "xc")
    return jax.shard_map(
        body,
        mesh=split,
        in_specs=(
            P(req, None),
            P(("page",) + req, None, None),
            P(("page",) + req, None, None),
            P(req, None),
            P(req),
        ),
        out_specs=P(req, "page"),
        check_vma=False,
    )
```

```python
import functools
import math

import jax
import jax.numpy as jnp
from jax import lax
from jax.experimental import pallas as pl
from jax.experimental.pallas import tpu as pltpu
from jax.sharding import Mesh
from jax.sharding import PartitionSpec as P

H = 64
KVH = 8
HD = 128
LANES = 128
STAT_ROWS = 8


def split_pair(value):
    high = lax.reduce_precision(value, exponent_bits=8, mantissa_bits=7)
    low = lax.reduce_precision(value - high, exponent_bits=8, mantissa_bits=7)
    return high, low


def score_kernel(q_ref, k_ref, hit_ref, w_ref, stat_ref):
    pages, page_len, _ = k_ref.shape
    q = q_ref[0]
    keys = k_ref[...].reshape(pages * page_len, HD)
    scores = lax.dot_general(
        q, keys, (((1,), (1,)), ((), ())), preferred_element_type=jnp.float32
    ) * (1.0 / math.sqrt(HD))
    req_rows = hit_ref.shape[0]
    groups = q.shape[0] // req_rows
    hit = jnp.concatenate([hit_ref[...]] * groups, axis=0) > 0.5
    scores = jnp.where(hit, scores, jnp.float32(-1e30))
    top = jnp.max(scores, axis=1, keepdims=True)
    high = top.astype(jnp.bfloat16).astype(jnp.float32)
    low = (top - high).astype(jnp.bfloat16).astype(jnp.float32)
    shift = high + low
    terms = jnp.where(hit, jnp.exp(scores - shift), jnp.float32(0.0))
    total = jnp.sum(terms, axis=1, keepdims=True)
    w_ref[0] = terms.astype(jnp.bfloat16)
    lane = lax.broadcasted_iota(jnp.int32, (q.shape[0], LANES), 1)
    stat_tile = jnp.where(
        lane == 0, high, jnp.where(lane == 1, low, jnp.where(lane == 2, total, 0.0))
    )
    stat_ref[0] = jnp.transpose(stat_tile)[: stat_ref.shape[1], :]


def mix_kernel(rows, own_heads, req_rows, w_ref, v_ref, out_ref):
    pages, page_len, _ = v_ref.shape
    values = v_ref[...].reshape(pages * page_len, HD)
    weights = w_ref[0]
    groups = weights.shape[0] // req_rows
    halves = req_rows // rows
    mixed = jnp.dot(weights, values, preferred_element_type=jnp.float32).astype(jnp.bfloat16)
    for g in range(groups):
        for y in range(halves):
            first = g * req_rows + y * rows
            block = (g // own_heads) * halves + y
            row = (g % own_heads) * rows
            out_ref[block, row : row + rows, :] = mixed[first : first + rows, :]


def attend(grouped_q, keys, values, token_hit, rows, own_heads):
    kv_heads, q_rows, _ = grouped_q.shape
    pages, page_len, _ = keys.shape
    tokens = pages * page_len
    req_rows = token_hit.shape[0]
    groups = q_rows // req_rows
    per_head_blocks = groups // own_heads * (req_rows // rows)
    block_rows = own_heads * rows
    kv_spec = pl.BlockSpec((pages, page_len, HD), lambda k: (0, 0, k))
    w_spec = pl.BlockSpec((1, q_rows, tokens), lambda k: (k, 0, 0))
    weights, stats = pl.pallas_call(
        score_kernel,
        grid=(kv_heads,),
        in_specs=[
            pl.BlockSpec((1, q_rows, HD), lambda k: (k, 0, 0)),
            kv_spec,
            pl.BlockSpec(token_hit.shape, lambda k: (0, 0)),
        ],
        out_specs=[w_spec, pl.BlockSpec((1, STAT_ROWS, q_rows), lambda k: (k, 0, 0))],
        out_shape=[
            jax.ShapeDtypeStruct((kv_heads, q_rows, tokens), jnp.bfloat16),
            jax.ShapeDtypeStruct((kv_heads, STAT_ROWS, q_rows), jnp.float32),
        ],
        cost_estimate=pl.CostEstimate(
            flops=2 * kv_heads * q_rows * tokens * HD,
            transcendentals=kv_heads * q_rows * tokens,
            bytes_accessed=2 * (grouped_q.size + keys.size + kv_heads * q_rows * tokens),
        ),
    )(grouped_q, keys, token_hit)
    out_blocks = pl.pallas_call(
        functools.partial(mix_kernel, rows, own_heads, req_rows),
        grid=(kv_heads,),
        in_specs=[w_spec, kv_spec],
        out_specs=pl.BlockSpec((per_head_blocks, block_rows, HD), lambda k: (k, 0, 0)),
        out_shape=jax.ShapeDtypeStruct((kv_heads * per_head_blocks, block_rows, HD), jnp.bfloat16),
        cost_estimate=pl.CostEstimate(
            flops=2 * kv_heads * q_rows * tokens * HD,
            transcendentals=0,
            bytes_accessed=2 * (values.size + kv_heads * q_rows * tokens + kv_heads * q_rows * HD),
        ),
    )(weights, values)
    return out_blocks, stats

def body(queries, key_pool, value_pool, page_table, page_count):
    n_page = lax.axis_size("page")
    n_yh = lax.axis_size("yh")
    n_xc = lax.axis_size("xc")
    page_index = lax.axis_index("page")
    yh_index = lax.axis_index("yh")
    pages_held = key_pool.shape[0]
    page_len = key_pool.shape[1]
    per_kv = H // KVH
    own_heads = H // n_page
    rows = queries.shape[0]
    score_scale = 1.0 / math.sqrt(HD)

    row_pages = n_yh * n_xc * pages_held
    row_ids = page_index * row_pages + jnp.arange(row_pages, dtype=jnp.int32)
    slot_live = jnp.arange(page_table.shape[1], dtype=jnp.int32)[None, :] < page_count[:, None]
    row_hit = jnp.any(
        (page_table[:, :, None] == row_ids[None, None, :]) & slot_live[:, :, None], axis=1
    )
    mask_cols = -(-row_pages // LANES) * LANES
    row_hit = jnp.pad(row_hit.astype(queries.dtype), ((0, 0), (0, mask_cols - row_pages)))
    packed = jnp.concatenate([queries, row_hit], axis=1)

    all_packed = lax.all_gather(packed, "yh", tiled=True)
    keys = lax.all_gather(key_pool, "xc", tiled=True)
    values = lax.all_to_all(
        jnp.broadcast_to(value_pool[None], (n_xc,) + value_pool.shape).reshape(
            (n_xc * pages_held,) + value_pool.shape[1:]
        ),
        "xc",
        0,
        0,
        tiled=True,
    )

    req_rows = all_packed.shape[0]
    all_q = all_packed[:, : H * HD]
    held = n_xc * pages_held
    page_hit = lax.dynamic_slice_in_dim(all_packed, H * HD + yh_index * held, held, 1) > 0.5
    token_hit = jnp.repeat(page_hit, page_len, axis=1).astype(jnp.float32)

    grouped = all_q.reshape(req_rows, KVH, per_kv, HD).transpose(1, 2, 0, 3)
    grouped = grouped.reshape(KVH, per_kv * req_rows, HD)
    n_blocks = n_page * n_yh
    block_rows = rows * own_heads
    out_blocks, stat_k = attend(grouped, keys, values, token_hit, rows, own_heads)
    stat_k = stat_k[:, :3, :].reshape(KVH, 3, per_kv // own_heads, own_heads, n_yh, rows)
    stat_k = stat_k.transpose(1, 0, 2, 4, 3, 5).reshape(3, n_blocks, block_rows)
    max_hi = stat_k[0]
    max_lo = stat_k[1]
    sum_hi, sum_lo = split_pair(stat_k[2])
    stat_cols = -(-4 * block_rows // HD) * HD
    stats = jnp.concatenate(
        [max_hi, max_lo, sum_hi, sum_lo]
        + [jnp.zeros((n_blocks, stat_cols - 4 * block_rows), jnp.float32)],
        axis=1,
    ).astype(jnp.bfloat16)
    payload = jnp.concatenate([out_blocks, stats.reshape(n_blocks, -1, HD)], axis=1)
    arrived = lax.all_to_all(payload, ("page", "yh"), 0, 0, tiled=True)

    part_out = arrived[:, :block_rows, :].astype(jnp.float32)
    part_stats = arrived[:, block_rows:, :].reshape(n_blocks, stat_cols).astype(jnp.float32)
    part_max = part_stats[:, :block_rows] + part_stats[:, block_rows : 2 * block_rows]
    part_sum = part_stats[:, 2 * block_rows : 3 * block_rows] + part_stats[:, 3 * block_rows : 4 * block_rows]
    joint_max = jnp.max(part_max, axis=0)
    factor = jnp.exp(part_max - joint_max[None, :])
    joint_sum = jnp.sum(part_sum * factor, axis=0)
    joint_out = jnp.sum(part_out * factor[..., None], axis=0)
    result = (joint_out / joint_sum[:, None]).reshape(own_heads, rows, HD).transpose(1, 0, 2)
    return result.reshape(rows, own_heads * HD).astype(jnp.bfloat16)


def solution(mesh):
    n_page, n_req = mesh.devices.shape
    n_yh = 2 if n_req % 2 == 0 else 1
    split = Mesh(mesh.devices.reshape(n_page, n_yh, n_req // n_yh), ("page", "yh", "xc"))
    req = ("yh", "xc")
    return jax.shard_map(
        body,
        mesh=split,
        in_specs=(
            P(req, None),
            P(("page",) + req, None, None),
            P(("page",) + req, None, None),
            P(req, None),
            P(req),
        ),
        out_specs=P(req, "page"),
        check_vma=False,
    )
```

```python
import functools
import math

import jax
import jax.numpy as jnp
from jax import lax
from jax.experimental import pallas as pl
from jax.experimental.pallas import tpu as pltpu
from jax.sharding import Mesh
from jax.sharding import PartitionSpec as P

H = 64
KVH = 8
HD = 128
LANES = 128
STAT_ROWS = 8
HEADS_PER_STEP = 2


def split_pair(value):
    high = lax.reduce_precision(value, exponent_bits=8, mantissa_bits=7)
    low = lax.reduce_precision(value - high, exponent_bits=8, mantissa_bits=7)
    return high, low


def attend_kernel(rows, own_heads, q_ref, k_ref, v_ref, hit_ref, out_ref, stat_ref):
    for step in range(q_ref.shape[0]):
        attend_head(rows, own_heads, step, q_ref, k_ref, v_ref, hit_ref, out_ref, stat_ref)


def attend_head(rows, own_heads, step, q_ref, k_ref, v_ref, hit_ref, out_ref, stat_ref):
    pages, page_len, _ = k_ref.shape
    q = q_ref[step]
    lanes = pl.ds(step * HD, HD)
    keys = k_ref[:, :, lanes].reshape(pages * page_len, HD)
    values = v_ref[:, :, lanes].reshape(pages * page_len, HD)
    scores = lax.dot_general(
        q, keys, (((1,), (1,)), ((), ())), preferred_element_type=jnp.float32
    ) * (1.0 / math.sqrt(HD))
    req_rows = hit_ref.shape[0]
    groups = q.shape[0] // req_rows
    halves = req_rows // rows
    hit = jnp.concatenate([hit_ref[...]] * groups, axis=0) > 0.5
    scores = jnp.where(hit, scores, jnp.float32(-1e30))
    top = jnp.max(scores, axis=1, keepdims=True)
    high = top.astype(jnp.bfloat16).astype(jnp.float32)
    low = (top - high).astype(jnp.bfloat16).astype(jnp.float32)
    shift = high + low
    terms = jnp.where(hit, jnp.exp(scores - shift), jnp.float32(0.0))
    total = jnp.sum(terms, axis=1, keepdims=True)
    mixed = jnp.dot(
        terms.astype(jnp.bfloat16), values, preferred_element_type=jnp.float32
    ).astype(jnp.bfloat16)
    base = step * (groups // own_heads) * halves
    for g in range(groups):
        for y in range(halves):
            first = g * req_rows + y * rows
            block = base + (g // own_heads) * halves + y
            row = (g % own_heads) * rows
            out_ref[block, row : row + rows, :] = mixed[first : first + rows, :]
    lane = lax.broadcasted_iota(jnp.int32, (q.shape[0], LANES), 1)
    stat_tile = jnp.where(
        lane == 0, high, jnp.where(lane == 1, low, jnp.where(lane == 2, total, 0.0))
    )
    stat_ref[step] = jnp.transpose(stat_tile)[: stat_ref.shape[1], :]


def attend(grouped_q, keys, values, token_hit, rows, own_heads):
    kv_heads, q_rows, _ = grouped_q.shape
    pages, page_len, _ = keys.shape
    tokens = pages * page_len
    req_rows = token_hit.shape[0]
    groups = q_rows // req_rows
    per_head_blocks = groups // own_heads * (req_rows // rows)
    block_rows = own_heads * rows
    return pl.pallas_call(
        functools.partial(attend_kernel, rows, own_heads),
        grid=(kv_heads // HEADS_PER_STEP,),
        in_specs=[
            pl.BlockSpec((HEADS_PER_STEP, q_rows, HD), lambda k: (k, 0, 0)),
            pl.BlockSpec((pages, page_len, HEADS_PER_STEP * HD), lambda k: (0, 0, k)),
            pl.BlockSpec((pages, page_len, HEADS_PER_STEP * HD), lambda k: (0, 0, k)),
            pl.BlockSpec(token_hit.shape, lambda k: (0, 0)),
        ],
        out_specs=[
            pl.BlockSpec((HEADS_PER_STEP * per_head_blocks, block_rows, HD), lambda k: (k, 0, 0)),
            pl.BlockSpec((HEADS_PER_STEP, STAT_ROWS, q_rows), lambda k: (k, 0, 0)),
        ],
        out_shape=[
            jax.ShapeDtypeStruct((kv_heads * per_head_blocks, block_rows, HD), jnp.bfloat16),
            jax.ShapeDtypeStruct((kv_heads, STAT_ROWS, q_rows), jnp.float32),
        ],
        cost_estimate=pl.CostEstimate(
            flops=4 * kv_heads * q_rows * tokens * HD,
            transcendentals=kv_heads * q_rows * tokens,
            bytes_accessed=2 * (grouped_q.size + keys.size + values.size) + 6 * kv_heads * q_rows * HD,
        ),
    )(grouped_q, keys, values, token_hit)

def body(queries, key_pool, value_pool, page_table, page_count):
    n_page = lax.axis_size("page")
    n_yh = lax.axis_size("yh")
    n_xc = lax.axis_size("xc")
    page_index = lax.axis_index("page")
    yh_index = lax.axis_index("yh")
    pages_held = key_pool.shape[0]
    page_len = key_pool.shape[1]
    per_kv = H // KVH
    own_heads = H // n_page
    rows = queries.shape[0]
    score_scale = 1.0 / math.sqrt(HD)

    row_pages = n_yh * n_xc * pages_held
    row_ids = page_index * row_pages + jnp.arange(row_pages, dtype=jnp.int32)
    slot_live = jnp.arange(page_table.shape[1], dtype=jnp.int32)[None, :] < page_count[:, None]
    row_hit = jnp.any(
        (page_table[:, :, None] == row_ids[None, None, :]) & slot_live[:, :, None], axis=1
    )
    mask_cols = -(-row_pages // LANES) * LANES
    row_hit = jnp.pad(row_hit.astype(queries.dtype), ((0, 0), (0, mask_cols - row_pages)))
    packed = jnp.concatenate([queries, row_hit], axis=1)

    all_packed = lax.all_gather(packed, "yh", tiled=True)
    keys = lax.all_gather(key_pool, "xc", tiled=True)
    values = lax.all_to_all(
        jnp.broadcast_to(value_pool[None], (n_xc,) + value_pool.shape).reshape(
            (n_xc * pages_held,) + value_pool.shape[1:]
        ),
        "xc",
        0,
        0,
        tiled=True,
    )

    req_rows = all_packed.shape[0]
    all_q = all_packed[:, : H * HD]
    held = n_xc * pages_held
    page_hit = lax.dynamic_slice_in_dim(all_packed, H * HD + yh_index * held, held, 1) > 0.5
    token_hit = jnp.repeat(page_hit, page_len, axis=1).astype(jnp.float32)

    grouped = all_q.reshape(req_rows, KVH, per_kv, HD).transpose(1, 2, 0, 3)
    grouped = grouped.reshape(KVH, per_kv * req_rows, HD)
    n_blocks = n_page * n_yh
    block_rows = rows * own_heads
    out_blocks, stat_k = attend(grouped, keys, values, token_hit, rows, own_heads)
    stat_k = stat_k[:, :3, :].reshape(KVH, 3, per_kv // own_heads, own_heads, n_yh, rows)
    stat_k = stat_k.transpose(1, 0, 2, 4, 3, 5).reshape(3, n_blocks, block_rows)
    max_hi = stat_k[0]
    max_lo = stat_k[1]
    sum_hi, sum_lo = split_pair(stat_k[2])
    stat_cols = -(-4 * block_rows // HD) * HD
    stats = jnp.concatenate(
        [max_hi, max_lo, sum_hi, sum_lo]
        + [jnp.zeros((n_blocks, stat_cols - 4 * block_rows), jnp.float32)],
        axis=1,
    ).astype(jnp.bfloat16)
    payload = jnp.concatenate([out_blocks, stats.reshape(n_blocks, -1, HD)], axis=1)
    arrived = lax.all_to_all(payload, ("page", "yh"), 0, 0, tiled=True)

    part_out = arrived[:, :block_rows, :].astype(jnp.float32)
    part_stats = arrived[:, block_rows:, :].reshape(n_blocks, stat_cols).astype(jnp.float32)
    part_max = part_stats[:, :block_rows] + part_stats[:, block_rows : 2 * block_rows]
    part_sum = part_stats[:, 2 * block_rows : 3 * block_rows] + part_stats[:, 3 * block_rows : 4 * block_rows]
    joint_max = jnp.max(part_max, axis=0)
    factor = jnp.exp(part_max - joint_max[None, :])
    joint_sum = jnp.sum(part_sum * factor, axis=0)
    joint_out = jnp.sum(part_out * factor[..., None], axis=0)
    result = (joint_out / joint_sum[:, None]).reshape(own_heads, rows, HD).transpose(1, 0, 2)
    return result.reshape(rows, own_heads * HD).astype(jnp.bfloat16)


def solution(mesh):
    n_page, n_req = mesh.devices.shape
    n_yh = 2 if n_req % 2 == 0 else 1
    split = Mesh(mesh.devices.reshape(n_page, n_yh, n_req // n_yh), ("page", "yh", "xc"))
    req = ("yh", "xc")
    return jax.shard_map(
        body,
        mesh=split,
        in_specs=(
            P(req, None),
            P(("page",) + req, None, None),
            P(("page",) + req, None, None),
            P(req, None),
            P(req),
        ),
        out_specs=P(req, "page"),
        check_vma=False,
    )
```

```python
import functools
import math

import jax
import jax.numpy as jnp
from jax import lax
from jax.experimental import pallas as pl
from jax.experimental.pallas import tpu as pltpu
from jax.sharding import Mesh
from jax.sharding import PartitionSpec as P

H = 64
KVH = 8
HD = 128
LANES = 128
STAT_ROWS = 8
HEADS_PER_STEP = 4


def split_pair(value):
    high = lax.reduce_precision(value, exponent_bits=8, mantissa_bits=7)
    low = lax.reduce_precision(value - high, exponent_bits=8, mantissa_bits=7)
    return high, low


def attend_kernel(rows, own_heads, q_ref, k_ref, v_ref, hit_ref, out_ref, stat_ref):
    for step in range(q_ref.shape[0]):
        attend_head(rows, own_heads, step, q_ref, k_ref, v_ref, hit_ref, out_ref, stat_ref)


def attend_head(rows, own_heads, step, q_ref, k_ref, v_ref, hit_ref, out_ref, stat_ref):
    pages, page_len, _ = k_ref.shape
    q = q_ref[step]
    lanes = pl.ds(step * HD, HD)
    keys = k_ref[:, :, lanes].reshape(pages * page_len, HD)
    values = v_ref[:, :, lanes].reshape(pages * page_len, HD)
    scores = lax.dot_general(
        q, keys, (((1,), (1,)), ((), ())), preferred_element_type=jnp.float32
    ) * (1.0 / math.sqrt(HD))
    req_rows = hit_ref.shape[0]
    groups = q.shape[0] // req_rows
    halves = req_rows // rows
    hit = jnp.concatenate([hit_ref[...]] * groups, axis=0) > 0.5
    scores = jnp.where(hit, scores, jnp.float32(-1e30))
    top = jnp.max(scores, axis=1, keepdims=True)
    high = top.astype(jnp.bfloat16).astype(jnp.float32)
    low = (top - high).astype(jnp.bfloat16).astype(jnp.float32)
    shift = high + low
    terms = jnp.where(hit, jnp.exp(scores - shift), jnp.float32(0.0))
    total = jnp.sum(terms, axis=1, keepdims=True)
    mixed = jnp.dot(
        terms.astype(jnp.bfloat16), values, preferred_element_type=jnp.float32
    ).astype(jnp.bfloat16)
    base = step * (groups // own_heads) * halves
    for g in range(groups):
        for y in range(halves):
            first = g * req_rows + y * rows
            block = base + (g // own_heads) * halves + y
            row = (g % own_heads) * rows
            out_ref[block, row : row + rows, :] = mixed[first : first + rows, :]
    lane = lax.broadcasted_iota(jnp.int32, (q.shape[0], LANES), 1)
    stat_tile = jnp.where(
        lane == 0, high, jnp.where(lane == 1, low, jnp.where(lane == 2, total, 0.0))
    )
    stat_ref[step] = jnp.transpose(stat_tile)[: stat_ref.shape[1], :]


def attend(grouped_q, keys, values, token_hit, rows, own_heads):
    kv_heads, q_rows, _ = grouped_q.shape
    pages, page_len, _ = keys.shape
    tokens = pages * page_len
    req_rows = token_hit.shape[0]
    groups = q_rows // req_rows
    per_head_blocks = groups // own_heads * (req_rows // rows)
    block_rows = own_heads * rows
    return pl.pallas_call(
        functools.partial(attend_kernel, rows, own_heads),
        grid=(kv_heads // HEADS_PER_STEP,),
        in_specs=[
            pl.BlockSpec((HEADS_PER_STEP, q_rows, HD), lambda k: (k, 0, 0)),
            pl.BlockSpec((pages, page_len, HEADS_PER_STEP * HD), lambda k: (0, 0, k)),
            pl.BlockSpec((pages, page_len, HEADS_PER_STEP * HD), lambda k: (0, 0, k)),
            pl.BlockSpec(token_hit.shape, lambda k: (0, 0)),
        ],
        out_specs=[
            pl.BlockSpec((HEADS_PER_STEP * per_head_blocks, block_rows, HD), lambda k: (k, 0, 0)),
            pl.BlockSpec((HEADS_PER_STEP, STAT_ROWS, q_rows), lambda k: (k, 0, 0)),
        ],
        out_shape=[
            jax.ShapeDtypeStruct((kv_heads * per_head_blocks, block_rows, HD), jnp.bfloat16),
            jax.ShapeDtypeStruct((kv_heads, STAT_ROWS, q_rows), jnp.float32),
        ],
        cost_estimate=pl.CostEstimate(
            flops=4 * kv_heads * q_rows * tokens * HD,
            transcendentals=kv_heads * q_rows * tokens,
            bytes_accessed=2 * (grouped_q.size + keys.size + values.size) + 6 * kv_heads * q_rows * HD,
        ),
    )(grouped_q, keys, values, token_hit)

def body(queries, key_pool, value_pool, page_table, page_count):
    n_page = lax.axis_size("page")
    n_yh = lax.axis_size("yh")
    n_xc = lax.axis_size("xc")
    page_index = lax.axis_index("page")
    yh_index = lax.axis_index("yh")
    pages_held = key_pool.shape[0]
    page_len = key_pool.shape[1]
    per_kv = H // KVH
    own_heads = H // n_page
    rows = queries.shape[0]
    score_scale = 1.0 / math.sqrt(HD)

    row_pages = n_yh * n_xc * pages_held
    row_ids = page_index * row_pages + jnp.arange(row_pages, dtype=jnp.int32)
    slot_live = jnp.arange(page_table.shape[1], dtype=jnp.int32)[None, :] < page_count[:, None]
    row_hit = jnp.any(
        (page_table[:, :, None] == row_ids[None, None, :]) & slot_live[:, :, None], axis=1
    )
    mask_cols = -(-row_pages // LANES) * LANES
    row_hit = jnp.pad(row_hit.astype(queries.dtype), ((0, 0), (0, mask_cols - row_pages)))
    packed = jnp.concatenate([queries, row_hit], axis=1)

    all_packed = lax.all_gather(packed, "yh", tiled=True)
    keys = lax.all_gather(key_pool, "xc", tiled=True)
    values = lax.all_to_all(
        jnp.broadcast_to(value_pool[None], (n_xc,) + value_pool.shape).reshape(
            (n_xc * pages_held,) + value_pool.shape[1:]
        ),
        "xc",
        0,
        0,
        tiled=True,
    )

    req_rows = all_packed.shape[0]
    all_q = all_packed[:, : H * HD]
    held = n_xc * pages_held
    page_hit = lax.dynamic_slice_in_dim(all_packed, H * HD + yh_index * held, held, 1) > 0.5
    token_hit = jnp.repeat(page_hit, page_len, axis=1).astype(jnp.float32)

    grouped = all_q.reshape(req_rows, KVH, per_kv, HD).transpose(1, 2, 0, 3)
    grouped = grouped.reshape(KVH, per_kv * req_rows, HD)
    n_blocks = n_page * n_yh
    block_rows = rows * own_heads
    out_blocks, stat_k = attend(grouped, keys, values, token_hit, rows, own_heads)
    stat_k = stat_k[:, :3, :].reshape(KVH, 3, per_kv // own_heads, own_heads, n_yh, rows)
    stat_k = stat_k.transpose(1, 0, 2, 4, 3, 5).reshape(3, n_blocks, block_rows)
    max_hi = stat_k[0]
    max_lo = stat_k[1]
    sum_hi, sum_lo = split_pair(stat_k[2])
    stat_cols = -(-4 * block_rows // HD) * HD
    stats = jnp.concatenate(
        [max_hi, max_lo, sum_hi, sum_lo]
        + [jnp.zeros((n_blocks, stat_cols - 4 * block_rows), jnp.float32)],
        axis=1,
    ).astype(jnp.bfloat16)
    payload = jnp.concatenate([out_blocks, stats.reshape(n_blocks, -1, HD)], axis=1)
    arrived = lax.all_to_all(payload, ("page", "yh"), 0, 0, tiled=True)

    part_out = arrived[:, :block_rows, :].astype(jnp.float32)
    part_stats = arrived[:, block_rows:, :].reshape(n_blocks, stat_cols).astype(jnp.float32)
    part_max = part_stats[:, :block_rows] + part_stats[:, block_rows : 2 * block_rows]
    part_sum = part_stats[:, 2 * block_rows : 3 * block_rows] + part_stats[:, 3 * block_rows : 4 * block_rows]
    joint_max = jnp.max(part_max, axis=0)
    factor = jnp.exp(part_max - joint_max[None, :])
    joint_sum = jnp.sum(part_sum * factor, axis=0)
    joint_out = jnp.sum(part_out * factor[..., None], axis=0)
    result = (joint_out / joint_sum[:, None]).reshape(own_heads, rows, HD).transpose(1, 0, 2)
    return result.reshape(rows, own_heads * HD).astype(jnp.bfloat16)


def solution(mesh):
    n_page, n_req = mesh.devices.shape
    n_yh = 2 if n_req % 2 == 0 else 1
    split = Mesh(mesh.devices.reshape(n_page, n_yh, n_req // n_yh), ("page", "yh", "xc"))
    req = ("yh", "xc")
    return jax.shard_map(
        body,
        mesh=split,
        in_specs=(
            P(req, None),
            P(("page",) + req, None, None),
            P(("page",) + req, None, None),
            P(req, None),
            P(req),
        ),
        out_specs=P(req, "page"),
        check_vma=False,
    )
```

```python
import functools
import math

import jax
import jax.numpy as jnp
from jax import lax
from jax.experimental import pallas as pl
from jax.experimental.pallas import tpu as pltpu
from jax.sharding import Mesh
from jax.sharding import PartitionSpec as P

H = 64
KVH = 8
HD = 128
LANES = 128
STAT_ROWS = 8
HEADS_PER_STEP = 2


def split_pair(value):
    high = lax.reduce_precision(value, exponent_bits=8, mantissa_bits=7)
    low = lax.reduce_precision(value - high, exponent_bits=8, mantissa_bits=7)
    return high, low


def attend_kernel(rows, own_heads, q_ref, k_ref, v_ref, hit_ref, out_ref, stat_ref):
    for step in range(q_ref.shape[0]):
        attend_head(rows, own_heads, step, q_ref, k_ref, v_ref, hit_ref, out_ref, stat_ref)


def attend_head(rows, own_heads, step, q_ref, k_ref, v_ref, hit_ref, out_ref, stat_ref):
    pages, page_len, _ = k_ref.shape
    q = q_ref[step]
    lanes = pl.ds(step * HD, HD)
    keys = k_ref[:, :, lanes].reshape(pages * page_len, HD)
    values = v_ref[:, :, lanes].reshape(pages * page_len, HD)
    scores = lax.dot_general(
        q, keys, (((1,), (1,)), ((), ())), preferred_element_type=jnp.float32
    ) * (1.0 / math.sqrt(HD))
    req_rows = hit_ref.shape[0]
    groups = q.shape[0] // req_rows
    halves = req_rows // rows
    hit = jnp.concatenate([hit_ref[...]] * groups, axis=0) > 0.5
    scores = jnp.where(hit, scores, jnp.float32(-1e30))
    top = jnp.max(scores, axis=1, keepdims=True)
    high = top.astype(jnp.bfloat16).astype(jnp.float32)
    low = (top - high).astype(jnp.bfloat16).astype(jnp.float32)
    shift = high + low
    terms = jnp.where(hit, jnp.exp(scores - shift), jnp.float32(0.0))
    total = jnp.sum(terms, axis=1, keepdims=True)
    mixed = jnp.dot(
        terms.astype(jnp.bfloat16), values, preferred_element_type=jnp.float32
    ).astype(jnp.bfloat16)
    base = step * (groups // own_heads) * halves
    for g in range(groups):
        for y in range(halves):
            first = g * req_rows + y * rows
            block = base + (g // own_heads) * halves + y
            row = (g % own_heads) * rows
            out_ref[block, row : row + rows, :] = mixed[first : first + rows, :]
    lane = lax.broadcasted_iota(jnp.int32, (q.shape[0], LANES), 1)
    stat_tile = jnp.where(
        lane == 0, high, jnp.where(lane == 1, low, jnp.where(lane == 2, total, 0.0))
    )
    stat_ref[step] = jnp.transpose(stat_tile)[: stat_ref.shape[1], :]


def attend(grouped_q, keys, values, token_hit, rows, own_heads):
    kv_heads, q_rows, _ = grouped_q.shape
    pages, page_len, _ = keys.shape
    tokens = pages * page_len
    req_rows = token_hit.shape[0]
    groups = q_rows // req_rows
    per_head_blocks = groups // own_heads * (req_rows // rows)
    block_rows = own_heads * rows
    return pl.pallas_call(
        functools.partial(attend_kernel, rows, own_heads),
        grid=(kv_heads // HEADS_PER_STEP,),
        in_specs=[
            pl.BlockSpec((HEADS_PER_STEP, q_rows, HD), lambda k: (k, 0, 0)),
            pl.BlockSpec((pages, page_len, HEADS_PER_STEP * HD), lambda k: (0, 0, k)),
            pl.BlockSpec((pages, page_len, HEADS_PER_STEP * HD), lambda k: (0, 0, k)),
            pl.BlockSpec(token_hit.shape, lambda k: (0, 0)),
        ],
        out_specs=[
            pl.BlockSpec((HEADS_PER_STEP * per_head_blocks, block_rows, HD), lambda k: (k, 0, 0)),
            pl.BlockSpec((HEADS_PER_STEP, STAT_ROWS, q_rows), lambda k: (k, 0, 0)),
        ],
        out_shape=[
            jax.ShapeDtypeStruct((kv_heads * per_head_blocks, block_rows, HD), jnp.bfloat16),
            jax.ShapeDtypeStruct((kv_heads, STAT_ROWS, q_rows), jnp.float32),
        ],
        cost_estimate=pl.CostEstimate(
            flops=4 * kv_heads * q_rows * tokens * HD,
            transcendentals=kv_heads * q_rows * tokens,
            bytes_accessed=2 * (grouped_q.size + keys.size + values.size) + 6 * kv_heads * q_rows * HD,
        ),
    )(grouped_q, keys, values, token_hit)

def spread(block, axis):
    count = lax.axis_size(axis)
    copies = jnp.broadcast_to(block[None], (count,) + block.shape)
    return lax.all_to_all(copies.reshape((count * block.shape[0],) + block.shape[1:]), axis, 0, 0, tiled=True)


def body(queries, key_pool, value_pool, page_table, page_count):
    n_page = lax.axis_size("page")
    n_yh = lax.axis_size("yh")
    n_x = lax.axis_size("x")
    n_core = lax.axis_size("core")
    n_xc = n_x * n_core
    page_index = lax.axis_index("page")
    yh_index = lax.axis_index("yh")
    pages_held = key_pool.shape[0]
    page_len = key_pool.shape[1]
    per_kv = H // KVH
    own_heads = H // n_page
    rows = queries.shape[0]
    score_scale = 1.0 / math.sqrt(HD)

    row_pages = n_yh * n_xc * pages_held
    row_ids = page_index * row_pages + jnp.arange(row_pages, dtype=jnp.int32)
    slot_live = jnp.arange(page_table.shape[1], dtype=jnp.int32)[None, :] < page_count[:, None]
    row_hit = jnp.any(
        (page_table[:, :, None] == row_ids[None, None, :]) & slot_live[:, :, None], axis=1
    )
    mask_cols = -(-row_pages // LANES) * LANES
    row_hit = jnp.pad(row_hit.astype(queries.dtype), ((0, 0), (0, mask_cols - row_pages)))
    packed = jnp.concatenate([queries, row_hit], axis=1)

    all_packed = lax.all_gather(packed, "yh", tiled=True)
    keys = lax.all_gather(lax.all_gather(key_pool, "x", tiled=True), "core", tiled=True)
    values = spread(spread(value_pool, "x"), "core")

    req_rows = all_packed.shape[0]
    all_q = all_packed[:, : H * HD]
    held = n_xc * pages_held
    page_hit = lax.dynamic_slice_in_dim(all_packed, H * HD + yh_index * held, held, 1) > 0.5
    order = [(x * n_core + c) * pages_held + j for c in range(n_core) for x in range(n_x) for j in range(pages_held)]
    page_hit = jnp.take(page_hit, jnp.asarray(order, dtype=jnp.int32), axis=1)
    token_hit = jnp.repeat(page_hit, page_len, axis=1).astype(jnp.float32)

    grouped = all_q.reshape(req_rows, KVH, per_kv, HD).transpose(1, 2, 0, 3)
    grouped = grouped.reshape(KVH, per_kv * req_rows, HD)
    n_blocks = n_page * n_yh
    block_rows = rows * own_heads
    out_blocks, stat_k = attend(grouped, keys, values, token_hit, rows, own_heads)
    stat_k = stat_k[:, :3, :].reshape(KVH, 3, per_kv // own_heads, own_heads, n_yh, rows)
    stat_k = stat_k.transpose(1, 0, 2, 4, 3, 5).reshape(3, n_blocks, block_rows)
    max_hi = stat_k[0]
    max_lo = stat_k[1]
    sum_hi, sum_lo = split_pair(stat_k[2])
    stat_cols = -(-4 * block_rows // HD) * HD
    stats = jnp.concatenate(
        [max_hi, max_lo, sum_hi, sum_lo]
        + [jnp.zeros((n_blocks, stat_cols - 4 * block_rows), jnp.float32)],
        axis=1,
    ).astype(jnp.bfloat16)
    payload = jnp.concatenate([out_blocks, stats.reshape(n_blocks, -1, HD)], axis=1)
    arrived = lax.all_to_all(payload, ("page", "yh"), 0, 0, tiled=True)

    part_out = arrived[:, :block_rows, :].astype(jnp.float32)
    part_stats = arrived[:, block_rows:, :].reshape(n_blocks, stat_cols).astype(jnp.float32)
    part_max = part_stats[:, :block_rows] + part_stats[:, block_rows : 2 * block_rows]
    part_sum = part_stats[:, 2 * block_rows : 3 * block_rows] + part_stats[:, 3 * block_rows : 4 * block_rows]
    joint_max = jnp.max(part_max, axis=0)
    factor = jnp.exp(part_max - joint_max[None, :])
    joint_sum = jnp.sum(part_sum * factor, axis=0)
    joint_out = jnp.sum(part_out * factor[..., None], axis=0)
    result = (joint_out / joint_sum[:, None]).reshape(own_heads, rows, HD).transpose(1, 0, 2)
    return result.reshape(rows, own_heads * HD).astype(jnp.bfloat16)


def solution(mesh):
    n_page, n_req = mesh.devices.shape
    n_yh = 2 if n_req % 4 == 0 else 1
    n_core = 2 if n_req % 2 == 0 else 1
    split = Mesh(
        mesh.devices.reshape(n_page, n_yh, n_req // (n_yh * n_core), n_core),
        ("page", "yh", "x", "core"),
    )
    req = ("yh", "x", "core")
    return jax.shard_map(
        body,
        mesh=split,
        in_specs=(
            P(req, None),
            P(("page",) + req, None, None),
            P(("page",) + req, None, None),
            P(req, None),
            P(req),
        ),
        out_specs=P(req, "page"),
        check_vma=False,
    )
```

```python
import functools
import math

import jax
import jax.numpy as jnp
from jax import lax
from jax.experimental import pallas as pl
from jax.experimental.pallas import tpu as pltpu
from jax.sharding import Mesh
from jax.sharding import PartitionSpec as P

H = 64
KVH = 8
HD = 128
LANES = 128
STAT_ROWS = 8
HEADS_PER_STEP = 2


def split_pair(value):
    high = lax.reduce_precision(value, exponent_bits=8, mantissa_bits=7)
    low = lax.reduce_precision(value - high, exponent_bits=8, mantissa_bits=7)
    return high, low


def attend_kernel(rows, own_heads, q_ref, k_ref, v_ref, hit_ref, out_ref, stat_ref):
    for step in range(q_ref.shape[0]):
        attend_head(rows, own_heads, step, q_ref, k_ref, v_ref, hit_ref, out_ref, stat_ref)


def attend_head(rows, own_heads, step, q_ref, k_ref, v_ref, hit_ref, out_ref, stat_ref):
    pages, page_len, _ = k_ref.shape
    q = q_ref[step]
    lanes = pl.ds(step * HD, HD)
    keys = k_ref[:, :, lanes].reshape(pages * page_len, HD)
    values = v_ref[:, :, lanes].reshape(pages * page_len, HD)
    scores = lax.dot_general(
        q, keys, (((1,), (1,)), ((), ())), preferred_element_type=jnp.float32
    ) * (1.0 / math.sqrt(HD))
    req_rows = hit_ref.shape[0]
    groups = q.shape[0] // req_rows
    halves = req_rows // rows
    hit = jnp.concatenate([hit_ref[...]] * groups, axis=0) > 0.5
    scores = jnp.where(hit, scores, jnp.float32(-1e30))
    top = jnp.max(scores, axis=1, keepdims=True)
    high = top.astype(jnp.bfloat16).astype(jnp.float32)
    low = (top - high).astype(jnp.bfloat16).astype(jnp.float32)
    shift = high + low
    terms = jnp.where(hit, jnp.exp(scores - shift), jnp.float32(0.0))
    total = jnp.sum(terms, axis=1, keepdims=True)
    mixed = jnp.dot(
        terms.astype(jnp.bfloat16), values, preferred_element_type=jnp.float32
    ).astype(jnp.bfloat16)
    base = step * (groups // own_heads) * halves
    for g in range(groups):
        for y in range(halves):
            first = g * req_rows + y * rows
            block = base + (g // own_heads) * halves + y
            row = (g % own_heads) * rows
            out_ref[block, row : row + rows, :] = mixed[first : first + rows, :]
    stat_rows = out_ref.shape[1] - own_heads * rows
    for block in range(base, base + (groups // own_heads) * halves):
        out_ref[block, own_heads * rows :, :] = jnp.zeros((stat_rows, HD), out_ref.dtype)
    lane = lax.broadcasted_iota(jnp.int32, (q.shape[0], LANES), 1)
    stat_tile = jnp.where(
        lane == 0, high, jnp.where(lane == 1, low, jnp.where(lane == 2, total, 0.0))
    )
    stat_ref[step] = jnp.transpose(stat_tile)[: stat_ref.shape[1], :]


def attend(grouped_q, keys, values, token_hit, rows, own_heads):
    kv_heads, q_rows, _ = grouped_q.shape
    pages, page_len, _ = keys.shape
    tokens = pages * page_len
    req_rows = token_hit.shape[0]
    groups = q_rows // req_rows
    per_head_blocks = groups // own_heads * (req_rows // rows)
    block_rows = own_heads * rows
    stat_rows = -(-4 * block_rows // HD)
    return pl.pallas_call(
        functools.partial(attend_kernel, rows, own_heads),
        grid=(kv_heads // HEADS_PER_STEP,),
        in_specs=[
            pl.BlockSpec((HEADS_PER_STEP, q_rows, HD), lambda k: (k, 0, 0)),
            pl.BlockSpec((pages, page_len, HEADS_PER_STEP * HD), lambda k: (0, 0, k)),
            pl.BlockSpec((pages, page_len, HEADS_PER_STEP * HD), lambda k: (0, 0, k)),
            pl.BlockSpec(token_hit.shape, lambda k: (0, 0)),
        ],
        out_specs=[
            pl.BlockSpec((HEADS_PER_STEP * per_head_blocks, block_rows + stat_rows, HD), lambda k: (k, 0, 0)),
            pl.BlockSpec((HEADS_PER_STEP, STAT_ROWS, q_rows), lambda k: (k, 0, 0)),
        ],
        out_shape=[
            jax.ShapeDtypeStruct((kv_heads * per_head_blocks, block_rows + stat_rows, HD), jnp.bfloat16),
            jax.ShapeDtypeStruct((kv_heads, STAT_ROWS, q_rows), jnp.float32),
        ],
        cost_estimate=pl.CostEstimate(
            flops=4 * kv_heads * q_rows * tokens * HD,
            transcendentals=kv_heads * q_rows * tokens,
            bytes_accessed=2 * (grouped_q.size + keys.size + values.size) + 6 * kv_heads * q_rows * HD,
        ),
    )(grouped_q, keys, values, token_hit)

def body(queries, key_pool, value_pool, page_table, page_count):
    n_page = lax.axis_size("page")
    n_yh = lax.axis_size("yh")
    n_xc = lax.axis_size("xc")
    page_index = lax.axis_index("page")
    yh_index = lax.axis_index("yh")
    pages_held = key_pool.shape[0]
    page_len = key_pool.shape[1]
    per_kv = H // KVH
    own_heads = H // n_page
    rows = queries.shape[0]
    score_scale = 1.0 / math.sqrt(HD)

    row_pages = n_yh * n_xc * pages_held
    row_ids = page_index * row_pages + jnp.arange(row_pages, dtype=jnp.int32)
    slot_live = jnp.arange(page_table.shape[1], dtype=jnp.int32)[None, :] < page_count[:, None]
    row_hit = jnp.any(
        (page_table[:, :, None] == row_ids[None, None, :]) & slot_live[:, :, None], axis=1
    )
    mask_cols = -(-row_pages // LANES) * LANES
    row_hit = jnp.pad(row_hit.astype(queries.dtype), ((0, 0), (0, mask_cols - row_pages)))
    packed = jnp.concatenate([queries, row_hit], axis=1)

    all_packed = lax.all_gather(packed, "yh", tiled=True)
    keys = lax.all_gather(key_pool, "xc", tiled=True)
    values = lax.all_to_all(
        jnp.broadcast_to(value_pool[None], (n_xc,) + value_pool.shape).reshape(
            (n_xc * pages_held,) + value_pool.shape[1:]
        ),
        "xc",
        0,
        0,
        tiled=True,
    )

    req_rows = all_packed.shape[0]
    all_q = all_packed[:, : H * HD]
    held = n_xc * pages_held
    page_hit = lax.dynamic_slice_in_dim(all_packed, H * HD + yh_index * held, held, 1) > 0.5
    token_hit = jnp.repeat(page_hit, page_len, axis=1).astype(jnp.float32)

    grouped = all_q.reshape(req_rows, KVH, per_kv, HD).transpose(1, 2, 0, 3)
    grouped = grouped.reshape(KVH, per_kv * req_rows, HD)
    n_blocks = n_page * n_yh
    block_rows = rows * own_heads
    out_blocks, stat_k = attend(grouped, keys, values, token_hit, rows, own_heads)
    stat_k = stat_k[:, :3, :].reshape(KVH, 3, per_kv // own_heads, own_heads, n_yh, rows)
    stat_k = stat_k.transpose(1, 0, 2, 4, 3, 5).reshape(3, n_blocks, block_rows)
    max_hi = stat_k[0]
    max_lo = stat_k[1]
    sum_hi, sum_lo = split_pair(stat_k[2])
    stat_cols = -(-4 * block_rows // HD) * HD
    stats = jnp.concatenate(
        [max_hi, max_lo, sum_hi, sum_lo]
        + [jnp.zeros((n_blocks, stat_cols - 4 * block_rows), jnp.float32)],
        axis=1,
    ).astype(jnp.bfloat16)
    payload = lax.dynamic_update_slice_in_dim(out_blocks, stats.reshape(n_blocks, -1, HD), block_rows, 1)
    arrived = lax.all_to_all(payload, ("page", "yh"), 0, 0, tiled=True)

    part_out = arrived[:, :block_rows, :].astype(jnp.float32)
    part_stats = arrived[:, block_rows:, :].reshape(n_blocks, stat_cols).astype(jnp.float32)
    part_max = part_stats[:, :block_rows] + part_stats[:, block_rows : 2 * block_rows]
    part_sum = part_stats[:, 2 * block_rows : 3 * block_rows] + part_stats[:, 3 * block_rows : 4 * block_rows]
    joint_max = jnp.max(part_max, axis=0)
    factor = jnp.exp(part_max - joint_max[None, :])
    joint_sum = jnp.sum(part_sum * factor, axis=0)
    joint_out = jnp.sum(part_out * factor[..., None], axis=0)
    result = (joint_out / joint_sum[:, None]).reshape(own_heads, rows, HD).transpose(1, 0, 2)
    return result.reshape(rows, own_heads * HD).astype(jnp.bfloat16)


def solution(mesh):
    n_page, n_req = mesh.devices.shape
    n_yh = 2 if n_req % 2 == 0 else 1
    split = Mesh(mesh.devices.reshape(n_page, n_yh, n_req // n_yh), ("page", "yh", "xc"))
    req = ("yh", "xc")
    return jax.shard_map(
        body,
        mesh=split,
        in_specs=(
            P(req, None),
            P(("page",) + req, None, None),
            P(("page",) + req, None, None),
            P(req, None),
            P(req),
        ),
        out_specs=P(req, "page"),
        check_vma=False,
    )
```
